256 devices in a mesh: req: 64 (over y, z, core), grp: 4 (over x).
Axes of the slice: x: 4, y: 4, z: 8, core: 2. Of those that a mesh axis runs over, the one named last changes fastest.
Arguments:
- hidden_in: bfloat16 [131072, 1280], P(('req', 'grp')), may hold values from -28 to 28
- queries: bfloat16 [131072, 1280], P(('req', 'grp')), may hold values from -20 to 20
- projected_keys: bfloat16 [131072, 320], P(('req', 'grp')), may hold values from -20 to 20
- projected_values: bfloat16 [131072, 320], P(('req', 'grp')), may hold values from -6 to 6
- segment: int32 [64, 4, 512], P('req', 'grp'), may hold values from 0 to 511, as said below
- live_rows: int32 [64, 4], P('req', 'grp'), may hold values from 0 to 512, as said below
- out_weight: bfloat16 [1280, 1280], replicated, may hold values from -0.15625 to 0.15625
- norm_gain: float32 [1280], replicated, may hold values from 0.5 to 1.5
- gate_weight: bfloat16 [1280, 3584], P(None, 'grp'), may hold values from -0.15625 to 0.15625
- up_weight: bfloat16 [1280, 3584], P(None, 'grp'), may hold values from -0.15625 to 0.15625
- down_weight: bfloat16 [3584, 1280], P('grp'), may hold values from -0.09375 to 0.09375
Outputs:
- layer_out: bfloat16 [131072, 1280], P(('req', 'grp'))
The draws below stay inside these ranges and needn't reach their ends.
Inputs may be any that keep to these rules, and one draw needn't show every extreme that they name: `live_rows`: in each group (one index of grp) the live rows of the 64 owners sum to exactly 8192, and one owner of each group has all 512 slots live. `segment`: within one owner the ids start at 0 at its first slot and rise by 0 or 1 from slot to slot.
All inputs are finite; a program needn't handle non-finite values.
Results may differ from the reference program's by a relative error of at most 0.008.
Values may be sent and summed in bfloat16 or wider, within the bound.
No kernel may reach another device: no remote copies, remote signals or barrier semaphores. Data moves between devices by JAX's collectives and lax.ppermute only.
A program may use at most 128 MiB of HBM per device.

```python
import math
import jax
import jax.numpy as jnp
from jax import lax

D = 1280
QUERY_HEADS = 20
KEY_VALUE_HEADS = 5
HEAD_SIZE = 64
FF = 3584
WINDOW = 128
SINK = 4
BAL = 128
OWNER_SLOTS = 512
TOTAL_SLOTS = 131072
N_REQ = 64
N_GRP = 4


def unmasked_field(key, shape):
    visible_field = jnp.clip(jax.random.normal(key, shape, jnp.float32), -4.5, 4.5)
    return visible_field


def draw_queries(key, part):
    visible_field = unmasked_field(jax.random.fold_in(key, 21), (TOTAL_SLOTS, QUERY_HEADS, HEAD_SIZE))
    return visible_field.reshape(TOTAL_SLOTS, QUERY_HEADS * HEAD_SIZE).astype(jnp.bfloat16)


def draw_projected_keys(key, part):
    visible_field = unmasked_field(jax.random.fold_in(key, 22), (TOTAL_SLOTS, KEY_VALUE_HEADS, HEAD_SIZE))
    return visible_field.reshape(TOTAL_SLOTS, KEY_VALUE_HEADS * HEAD_SIZE).astype(jnp.bfloat16)


def draw_hidden_in(key, part):
    first = jax.random.fold_in(jax.random.fold_in(key, 31), 0)
    visible_field = jnp.clip(jax.random.normal(first, (TOTAL_SLOTS, D), jnp.float32), -4.5, 4.5)
    return visible_field.astype(jnp.bfloat16)


def draw_segment(key, part):
    first, second, third, fourth = jax.random.split(jax.random.fold_in(key, 41), 4)
    periods = jnp.array([4, 32, 4096], dtype=jnp.int32)
    choose = jax.random.randint(first, (N_REQ, N_GRP, 1), 0, 3)
    period = jnp.sum(jnp.where(choose == jnp.arange(3, dtype=jnp.int32), periods, 0), axis=-1, keepdims=True)
    draws = jax.random.randint(second, (N_REQ, N_GRP, OWNER_SLOTS), 0, 1 << 30)
    flags = draws % period == 0
    flags = flags | (jnp.arange(OWNER_SLOTS, dtype=jnp.int32) == 0)[None, None, :]
    single_req = jax.random.randint(third, (), 0, N_REQ)
    single_grp = jax.random.randint(fourth, (), 0, N_GRP)
    req_ids = jnp.arange(N_REQ, dtype=jnp.int32)[:, None, None]
    grp_ids = jnp.arange(N_GRP, dtype=jnp.int32)[None, :, None]
    singles = (req_ids == single_req) & (grp_ids == single_grp)
    flags = flags | singles
    return (jnp.cumsum(flags.astype(jnp.int32), axis=-1) - 1).astype(jnp.int32)


def draw_live_rows(key, part):
    first, second, third = jax.random.split(jax.random.fold_in(key, 51), 3)
    quads = N_REQ // 4
    cuts = jnp.sort(jax.random.randint(first, (N_GRP, quads, 3), 0, 4 * BAL + 1), axis=-1)
    lower = jnp.zeros((N_GRP, quads, 1), jnp.int32)
    upper = jnp.full((N_GRP, quads, 1), 4 * BAL, jnp.int32)
    edges = jnp.concatenate([lower, cuts.astype(jnp.int32), upper], axis=-1)
    shares = edges[..., 1:] - edges[..., :-1]
    full_quad = jax.random.randint(second, (N_GRP, 1, 1), 0, quads)
    single = jnp.where(jnp.arange(4, dtype=jnp.int32) == 0, OWNER_SLOTS, 0).astype(jnp.int32)
    shares = jnp.where(jnp.arange(quads, dtype=jnp.int32)[None, :, None] == full_quad, single[None, None, :], shares)
    flat = shares.reshape(N_GRP, N_REQ)

    def shuffle(one_key):
        return jax.random.permutation(one_key, N_REQ)
    orders = jax.vmap(shuffle)(jax.random.split(third, N_GRP))
    placed = jnp.take_along_axis(flat, orders.astype(jnp.int32), axis=1)
    return jnp.transpose(placed).astype(jnp.int32)


def steps_of(key, shape, cuts, least, high):
    factor_of, own = 1.0, jax.random.fold_in(key, 6)
    for dim, parts in cuts:
        steps = jnp.exp(jax.random.uniform(jax.random.fold_in(own, dim), (parts,), jnp.float32, least / len(cuts), high / len(cuts)))
        factor_of = factor_of * jnp.repeat(steps, shape[dim] // parts).reshape([-1 if axis == dim else 1 for axis in range(len(shape))])
    return factor_of


def bell_draw(key, shape, scale, limit, shards=(), kind=jnp.bfloat16):
    level = steps_of(key, shape, shards, -0.22, 0.18) if shards else 1.0
    entries = jax.random.normal(key, shape, jnp.float32) * scale * level
    return jnp.minimum(jnp.maximum(entries, -limit), limit).astype(kind)


def setup_inputs(seed: int = 0) -> dict:
    key_list = jax.random.split(jax.random.key(seed), 12)
    return {
        "hidden_in": draw_hidden_in(jax.random.fold_in(key_list[11], 71), 0),
        "queries": draw_queries(jax.random.fold_in(key_list[11], 71), 0),
        "projected_keys": draw_projected_keys(jax.random.fold_in(key_list[11], 71), 0),
        "projected_values": bell_draw(key_list[3], (TOTAL_SLOTS, KEY_VALUE_HEADS * HEAD_SIZE), 1.0, 6.0, ((0, 256),)),
        "segment": draw_segment(jax.random.fold_in(key_list[11], 71), 0),
        "live_rows": draw_live_rows(jax.random.fold_in(key_list[11], 71), 0),
        "out_weight": bell_draw(key_list[6], (D, D), D ** -0.5, 0.15625),
        "norm_gain": jnp.clip(1.0 + 0.1 * jax.random.normal(key_list[7], (D,), jnp.float32), 0.5, 1.5),
        "gate_weight": bell_draw(key_list[8], (D, FF), D ** -0.5, 0.15625, ((1, 4),)),
        "up_weight": bell_draw(key_list[9], (D, FF), D ** -0.5, 0.15625, ((1, 4),)),
        "down_weight": bell_draw(key_list[10], (FF, D), FF ** -0.5, 0.09375, ((0, 4),)),
    }


rope_base = 10000.0
norm_eps = 1e-05

def apply_rotary(table, token_position):
    half = table.shape[-1] // 2
    inverse = rope_base ** (-(2.0 * jnp.arange(half, dtype=jnp.float32)) / table.shape[-1])
    angle = token_position.astype(jnp.float32)[:, None] * inverse[None, :]
    cosine = jnp.concatenate([jnp.cos(angle), jnp.cos(angle)], axis=-1)[:, None, :]
    sine = jnp.concatenate([jnp.sin(angle), jnp.sin(angle)], axis=-1)[:, None, :]
    numbers = table.astype(jnp.float32)
    turned = jnp.concatenate([-numbers[..., half:], numbers[..., :half]], axis=-1)
    return numbers * cosine + turned * sine

def attend(queries, projected_keys, projected_values, segment):
    slot_capacity = queries.shape[0]
    slots = jnp.arange(slot_capacity, dtype=jnp.int32)
    begins = jnp.concatenate([jnp.ones((1,), dtype=jnp.bool_), segment[1:] != segment[:-1]])
    starts = lax.cummax(jnp.where(begins, slots, 0).astype(jnp.int32), axis=0)
    token_position = slots - starts
    head_group = QUERY_HEADS // KEY_VALUE_HEADS
    query_rotated = apply_rotary(queries.reshape(slot_capacity, QUERY_HEADS, HEAD_SIZE), token_position).astype(jnp.bfloat16).reshape(slot_capacity, KEY_VALUE_HEADS, head_group, HEAD_SIZE)
    key_rotated = apply_rotary(projected_keys.reshape(slot_capacity, KEY_VALUE_HEADS, HEAD_SIZE), token_position).astype(jnp.bfloat16)
    scores = jnp.einsum('qngd,knd->ngqk', query_rotated.astype(jnp.float32), key_rotated.astype(jnp.float32)) / math.sqrt(HEAD_SIZE)
    allowed = (segment[:, None] == segment[None, :]) & (slots[None, :] <= slots[:, None])
    allowed = allowed & ((slots[:, None] - slots[None, :] < WINDOW) | (token_position[None, :] < SINK))
    scores = jnp.where(allowed, scores, -jnp.inf)
    largest = lax.optimization_barrier(jnp.max(scores, axis=-1, keepdims=True))
    raised = jnp.exp(scores - largest)
    layer_weights = (raised / lax.optimization_barrier(jnp.sum(raised, axis=-1, keepdims=True))).astype(jnp.bfloat16)
    attended_context = jnp.einsum('hemz,zhc->mhec', layer_weights.astype(jnp.float32), projected_values.reshape(slot_capacity, KEY_VALUE_HEADS, HEAD_SIZE).astype(jnp.float32))
    return attended_context.reshape(slot_capacity, QUERY_HEADS * HEAD_SIZE).astype(jnp.bfloat16)

def normalize(rows, norm_gain):
    numbers = rows.astype(jnp.float32)
    factor = lax.rsqrt(lax.optimization_barrier(jnp.mean(numbers * numbers, axis=-1, keepdims=True)) + norm_eps)
    return (numbers * factor * norm_gain.astype(jnp.float32)[None, :]).astype(jnp.bfloat16)

def reference(hidden_in, queries, projected_keys, projected_values, segment, live_rows, out_weight, norm_gain, gate_weight, up_weight, down_weight):
    request_owners = N_REQ * N_GRP

    def single_owner(pieces):
        return attend(pieces[0], pieces[1], pieces[2], pieces[3])
    attended_context = lax.map(single_owner, (queries.reshape(request_owners, OWNER_SLOTS, QUERY_HEADS * HEAD_SIZE), projected_keys.reshape(request_owners, OWNER_SLOTS, KEY_VALUE_HEADS * HEAD_SIZE), projected_values.reshape(request_owners, OWNER_SLOTS, KEY_VALUE_HEADS * HEAD_SIZE), segment.reshape(request_owners, OWNER_SLOTS)))
    attended_context = attended_context.reshape(TOTAL_SLOTS, QUERY_HEADS * HEAD_SIZE)
    mixed = (hidden_in.astype(jnp.float32) + jnp.dot(attended_context, out_weight, preferred_element_type=jnp.float32)).astype(jnp.bfloat16)
    keep = (jnp.arange(OWNER_SLOTS, dtype=jnp.int32)[None, :] < live_rows.reshape(request_owners, 1)).reshape(TOTAL_SLOTS)
    order = jnp.argsort(jnp.where(keep, 0, 1).astype(jnp.int32), stable=True).astype(jnp.int32)[:BAL * request_owners]
    rows = mixed[order]
    normed = normalize(rows, norm_gain)
    gate = jnp.dot(normed, gate_weight, preferred_element_type=jnp.float32)
    upward = jnp.dot(normed, up_weight, preferred_element_type=jnp.float32)
    hidden = (jax.nn.silu(gate) * upward).astype(jnp.bfloat16)
    width = FF // N_GRP
    total = jnp.zeros((BAL * request_owners, D), jnp.float32)
    for block in range(N_GRP):
        term = jnp.dot(hidden[:, block * width:(block + 1) * width], down_weight[block * width:(block + 1) * width], preferred_element_type=jnp.float32)
        total = total + lax.optimization_barrier(term.astype(jnp.bfloat16)).astype(jnp.float32)
    result = (rows.astype(jnp.float32) + total).astype(jnp.bfloat16)
    return jnp.zeros((TOTAL_SLOTS, D), jnp.bfloat16).at[order].set(result)
```

```python
import math

import jax
import jax.numpy as jnp
from jax import lax
from jax.experimental import pallas as pl
from jax.experimental.pallas import tpu as pltpu
from jax.sharding import PartitionSpec as P

QUERY_HEADS = 20
KEY_VALUE_HEADS = 5
HEAD_SIZE = 64
WINDOW = 128
SINK = 4
BAL = 128


rope_base = 10000.0
norm_eps = 1e-05
LANES = 128


def rotation_tables(token_position):
    half = HEAD_SIZE // 2
    inverse = rope_base ** (-(2.0 * jnp.arange(half, dtype=jnp.float32)) / HEAD_SIZE)
    angle = token_position.astype(jnp.float32)[:, None] * inverse[None, :]
    reps = LANES // half
    return jnp.tile(jnp.cos(angle), (1, reps)), jnp.tile(jnp.sin(angle), (1, reps))


def half_turn_matrix():
    lane = jnp.arange(LANES, dtype=jnp.int32)
    local = lane % HEAD_SIZE
    half = HEAD_SIZE // 2
    src = jnp.where(local < half, lane + half, lane - half)
    sign = jnp.where(local < half, -1.0, 1.0)
    turn = jnp.where(lane[:, None] == src[None, :], sign[None, :], 0.0)
    return turn.astype(jnp.bfloat16)


def attention_kernel(q_ref, k_ref, v_ref, cos_ref, sin_ref, turn_ref, segc_ref, segr_ref, posr_ref, out_ref, bias_ref):
    slots = q_ref.shape[0]
    block = LANES

    @pl.when(pl.program_id(0) == 0)
    def _():
        qi = lax.broadcasted_iota(jnp.int32, (slots, slots), 0)
        ki = lax.broadcasted_iota(jnp.int32, (slots, slots), 1)
        allowed = (segc_ref[...] == segr_ref[...]) & (ki <= qi)
        allowed = allowed & ((qi - ki < WINDOW) | (posr_ref[...] < SINK))
        bias_ref[...] = jnp.where(allowed, 0.0, -jnp.inf).astype(jnp.float32)

    cosine = cos_ref[...]
    sine = sin_ref[...]
    turn = turn_ref[...]

    def rotate(x):
        turned = jnp.dot(x, turn, preferred_element_type=jnp.float32)
        return (x.astype(jnp.float32) * cosine + turned * sine).astype(jnp.bfloat16)

    q_rot = rotate(q_ref[...])
    k_rot = rotate(k_ref[...])
    v = v_ref[...]
    lane = lax.broadcasted_iota(jnp.int32, (1, LANES), 1)
    low = lane < HEAD_SIZE
    zero = jnp.zeros((), jnp.bfloat16)
    q_low = jnp.where(low, q_rot, zero)
    q_high = jnp.where(low, zero, q_rot)
    scale = 1.0 / math.sqrt(HEAD_SIZE)
    for i in range(slots // block):
        keys = block * (i + 1)
        k_part = k_rot[:keys]
        v_part = v[:keys]
        bias = bias_ref[i * block:(i + 1) * block, :keys]
        parts = []
        for qh in (q_low, q_high):
            scores = lax.dot_general(
                qh[i * block:(i + 1) * block], k_part, (((1,), (1,)), ((), ())),
                preferred_element_type=jnp.float32,
            )
            scores = scores * scale + bias
            largest = jnp.max(scores, axis=-1, keepdims=True)
            raised = jnp.exp(scores - largest)
            total = jnp.sum(raised, axis=-1, keepdims=True)
            weights = (raised * (1.0 / total)).astype(jnp.bfloat16)
            parts.append(jnp.dot(weights, v_part, preferred_element_type=jnp.float32))
        context = jnp.where(low, parts[0], parts[1])
        out_ref[i * block:(i + 1) * block, :] = context.astype(out_ref.dtype)


def attend(queries, projected_keys, projected_values, segment):
    slot_capacity = queries.shape[0]
    slots = jnp.arange(slot_capacity, dtype=jnp.int32)
    begins = jnp.concatenate([jnp.ones((1,), dtype=jnp.bool_), segment[1:] != segment[:-1]])
    starts = lax.cummax(jnp.where(begins, slots, 0), axis=0)
    token_position = slots - starts
    cosine, sine = rotation_tables(token_position)
    turn = half_turn_matrix()
    def doubled(x):
        x = x.reshape(slot_capacity, KEY_VALUE_HEADS, 1, HEAD_SIZE)
        x = jnp.broadcast_to(x, (slot_capacity, KEY_VALUE_HEADS, 2, HEAD_SIZE))
        return x.reshape(slot_capacity, KEY_VALUE_HEADS * 2 * HEAD_SIZE)
    keys2 = doubled(projected_keys)
    values2 = doubled(projected_values)
    tiles = QUERY_HEADS * HEAD_SIZE // LANES
    per_kv = tiles // KEY_VALUE_HEADS
    full = lambda t: (0, 0)
    return pl.pallas_call(
        attention_kernel,
        grid=(tiles,),
        in_specs=[
            pl.BlockSpec((slot_capacity, LANES), lambda t: (0, t)),
            pl.BlockSpec((slot_capacity, LANES), lambda t: (0, t // per_kv)),
            pl.BlockSpec((slot_capacity, LANES), lambda t: (0, t // per_kv)),
            pl.BlockSpec((slot_capacity, LANES), full),
            pl.BlockSpec((slot_capacity, LANES), full),
            pl.BlockSpec((LANES, LANES), full),
            pl.BlockSpec((slot_capacity, 1), full),
            pl.BlockSpec((1, slot_capacity), full),
            pl.BlockSpec((1, slot_capacity), full),
        ],
        out_specs=pl.BlockSpec((slot_capacity, LANES), lambda t: (0, t)),
        out_shape=jax.ShapeDtypeStruct((slot_capacity, QUERY_HEADS * HEAD_SIZE), jnp.bfloat16),
        scratch_shapes=[pltpu.VMEM((slot_capacity, slot_capacity), jnp.float32)],
        compiler_params=pltpu.CompilerParams(dimension_semantics=("arbitrary",)),
    )(
        queries, keys2, values2, cosine, sine, turn,
        segment.reshape(slot_capacity, 1), segment.reshape(1, slot_capacity),
        token_position.reshape(1, slot_capacity),
    )


def normalize(rows, norm_gain):
    numbers = rows.astype(jnp.float32)
    factor = lax.rsqrt(jnp.mean(numbers * numbers, axis=-1, keepdims=True) + norm_eps)
    return (numbers * factor * norm_gain[None, :]).astype(jnp.bfloat16)


def project(attended_context, hidden_in, out_weight):
    return (
        hidden_in.astype(jnp.float32)
        + jnp.dot(attended_context, out_weight, preferred_element_type=jnp.float32)
    ).astype(jnp.bfloat16)


def feed_forward(normed, gate_weight, up_weight, down_weight):
    gathered = lax.all_gather(normed, "grp", axis=0, tiled=True)
    gate = jnp.dot(gathered, gate_weight, preferred_element_type=jnp.float32)
    upward = jnp.dot(gathered, up_weight, preferred_element_type=jnp.float32)
    hidden = (jax.nn.silu(gate) * upward).astype(jnp.bfloat16)
    return lax.psum_scatter(
        jnp.dot(hidden, down_weight, preferred_element_type=jnp.float32).astype(jnp.bfloat16),
        "grp",
        scatter_dimension=0,
        tiled=True,
    ).astype(jnp.float32)


def on_device(
    hidden_in,
    queries,
    projected_keys,
    projected_values,
    segment,
    live_rows,
    out_weight,
    norm_gain,
    gate_weight,
    up_weight,
    down_weight,
):
    slot_capacity = hidden_in.shape[0]
    attended_context = attend(
        queries, projected_keys, projected_values, segment.reshape(slot_capacity)
    )
    slots = jnp.arange(slot_capacity, dtype=jnp.int32)
    own_count = live_rows.reshape(())
    request_owners = lax.axis_size("req")
    own_index = lax.axis_index("req")
    block_rows = slot_capacity // request_owners
    counts = lax.all_to_all(
        jnp.broadcast_to(live_rows.reshape(1, 1), (request_owners, LANES)), "req", 0, 0, tiled=True
    )[:, 0]
    ends = jnp.cumsum(counts)
    firsts = ends - counts
    owner_ids = jnp.arange(request_owners, dtype=jnp.int32)
    own_first = jnp.sum(jnp.where(owner_ids == own_index, firsts, 0))
    own_shift = own_first % request_owners
    keep = slots < own_count
    stream = jnp.arange(BAL, dtype=jnp.int32) * request_owners + own_index
    source = jnp.sum((ends[None, :] <= stream[:, None]).astype(jnp.int32), axis=1)
    source_first = jnp.sum(
        jnp.where(source[:, None] == owner_ids[None, :], firsts[None, :], 0), axis=1
    )
    pick = (stream - source_first) // request_owners * request_owners + source
    rows = project(attended_context, hidden_in, out_weight)
    kept = jnp.where(keep[:, None], rows, jnp.zeros_like(rows))
    arrived = lax.all_to_all(
        jnp.roll(kept.reshape(block_rows, request_owners, rows.shape[1]), own_shift, axis=1),
        "req",
        split_axis=1,
        concat_axis=1,
        tiled=True,
    )
    mixed = arrived.reshape(slot_capacity, -1)[pick]
    normed = normalize(mixed, norm_gain)
    result = (
        mixed.astype(jnp.float32) + feed_forward(normed, gate_weight, up_weight, down_weight)
    ).astype(jnp.bfloat16)
    lanes = (own_index - firsts) % request_owners
    source_row = jnp.arange(block_rows, dtype=jnp.int32)[:, None] * request_owners + lanes[None, :]
    valid = source_row < counts[None, :]
    target = jnp.where(valid, (firsts[None, :] + source_row) // request_owners, 0)
    outgoing = jnp.where(valid[:, :, None], result[target], jnp.zeros((), jnp.bfloat16))
    returned = lax.all_to_all(outgoing, "req", split_axis=1, concat_axis=1, tiled=True)
    return jnp.roll(returned, -own_shift, axis=1).reshape(slot_capacity, -1)


def solution(mesh):
    placed = (
        P(("req", "grp"), None),
        P(("req", "grp"), None),
        P(("req", "grp"), None),
        P(("req", "grp"), None),
        P("req", "grp", None),
        P("req", "grp"),
        P(),
        P(),
        P(None, "grp"),
        P(None, "grp"),
        P("grp", None),
    )
    return jax.shard_map(
        on_device, mesh=mesh, in_specs=placed, out_specs=P(("req", "grp"), None), check_vma=False
    )
```

```python
import math

import jax
import jax.numpy as jnp
from jax import lax
from jax.experimental import pallas as pl
from jax.experimental.pallas import tpu as pltpu
from jax.sharding import PartitionSpec as P

QUERY_HEADS = 20
KEY_VALUE_HEADS = 5
HEAD_SIZE = 64
WINDOW = 128
SINK = 4
BAL = 128


rope_base = 10000.0
norm_eps = 1e-05
LANES = 128


def rotation_tables(token_position):
    half = HEAD_SIZE // 2
    inverse = rope_base ** (-(2.0 * jnp.arange(half, dtype=jnp.float32)) / HEAD_SIZE)
    angle = token_position.astype(jnp.float32)[:, None] * inverse[None, :]
    reps = LANES // half
    return jnp.tile(jnp.cos(angle), (1, reps)), jnp.tile(jnp.sin(angle), (1, reps))


def half_turn_matrix():
    lane = jnp.arange(LANES, dtype=jnp.int32)
    local = lane % HEAD_SIZE
    half = HEAD_SIZE // 2
    src = jnp.where(local < half, lane + half, lane - half)
    sign = jnp.where(local < half, -1.0, 1.0)
    turn = jnp.where(lane[:, None] == src[None, :], sign[None, :], 0.0)
    return turn.astype(jnp.bfloat16)


def attention_kernel(q_ref, k_ref, v_ref, cos_ref, sin_ref, turn_ref, segc_ref, segr_ref, posr_ref, out_ref, bias_ref):
    slots = q_ref.shape[0]
    block = LANES

    @pl.when(pl.program_id(0) == 0)
    def _():
        qi = lax.broadcasted_iota(jnp.int32, (slots, slots), 0)
        ki = lax.broadcasted_iota(jnp.int32, (slots, slots), 1)
        allowed = (segc_ref[...] == segr_ref[...]) & (ki <= qi)
        allowed = allowed & ((qi - ki < WINDOW) | (posr_ref[...] < SINK))
        bias_ref[...] = jnp.where(allowed, 0.0, -jnp.inf).astype(jnp.float32)

    cosine = cos_ref[...]
    sine = sin_ref[...]
    turn = turn_ref[...]

    def rotate(x):
        turned = jnp.dot(x, turn, preferred_element_type=jnp.float32)
        return (x.astype(jnp.float32) * cosine + turned * sine).astype(jnp.bfloat16)

    q_rot = rotate(q_ref[...])
    k_rot = rotate(k_ref[...])
    v = v_ref[...]
    lane = lax.broadcasted_iota(jnp.int32, (1, LANES), 1)
    low = lane < HEAD_SIZE
    zero = jnp.zeros((), jnp.bfloat16)
    q_low = jnp.where(low, q_rot, zero)
    q_high = jnp.where(low, zero, q_rot)
    scale = 1.0 / math.sqrt(HEAD_SIZE)
    for i in range(slots // block):
        keys = block * (i + 1)
        k_part = k_rot[:keys]
        v_part = v[:keys]
        bias = bias_ref[i * block:(i + 1) * block, :keys]
        parts = []
        for qh in (q_low, q_high):
            scores = lax.dot_general(
                qh[i * block:(i + 1) * block], k_part, (((1,), (1,)), ((), ())),
                preferred_element_type=jnp.float32,
            )
            scores = scores * scale + bias
            largest = jnp.max(scores, axis=-1, keepdims=True)
            raised = jnp.exp(scores - largest)
            total = jnp.sum(raised, axis=-1, keepdims=True)
            weights = (raised * (1.0 / total)).astype(jnp.bfloat16)
            parts.append(jnp.dot(weights, v_part, preferred_element_type=jnp.float32))
        context = jnp.where(low, parts[0], parts[1])
        out_ref[i * block:(i + 1) * block, :] = context.astype(out_ref.dtype)


def attend(queries, projected_keys, projected_values, segment):
    slot_capacity = queries.shape[0]
    slots = jnp.arange(slot_capacity, dtype=jnp.int32)
    begins = jnp.concatenate([jnp.ones((1,), dtype=jnp.bool_), segment[1:] != segment[:-1]])
    starts = lax.cummax(jnp.where(begins, slots, 0), axis=0)
    token_position = slots - starts
    cosine, sine = rotation_tables(token_position)
    turn = half_turn_matrix()
    def doubled(x):
        x = x.reshape(slot_capacity, KEY_VALUE_HEADS, 1, HEAD_SIZE)
        x = jnp.broadcast_to(x, (slot_capacity, KEY_VALUE_HEADS, 2, HEAD_SIZE))
        return x.reshape(slot_capacity, KEY_VALUE_HEADS * 2 * HEAD_SIZE)
    keys2 = doubled(projected_keys)
    values2 = doubled(projected_values)
    tiles = QUERY_HEADS * HEAD_SIZE // LANES
    per_kv = tiles // KEY_VALUE_HEADS
    full = lambda t: (0, 0)
    return pl.pallas_call(
        attention_kernel,
        grid=(tiles,),
        in_specs=[
            pl.BlockSpec((slot_capacity, LANES), lambda t: (0, t)),
            pl.BlockSpec((slot_capacity, LANES), lambda t: (0, t // per_kv)),
            pl.BlockSpec((slot_capacity, LANES), lambda t: (0, t // per_kv)),
            pl.BlockSpec((slot_capacity, LANES), full),
            pl.BlockSpec((slot_capacity, LANES), full),
            pl.BlockSpec((LANES, LANES), full),
            pl.BlockSpec((slot_capacity, 1), full),
            pl.BlockSpec((1, slot_capacity), full),
            pl.BlockSpec((1, slot_capacity), full),
        ],
        out_specs=pl.BlockSpec((slot_capacity, LANES), lambda t: (0, t)),
        out_shape=jax.ShapeDtypeStruct((slot_capacity, QUERY_HEADS * HEAD_SIZE), jnp.bfloat16),
        scratch_shapes=[pltpu.VMEM((slot_capacity, slot_capacity), jnp.float32)],
        compiler_params=pltpu.CompilerParams(dimension_semantics=("arbitrary",)),
    )(
        queries, keys2, values2, cosine, sine, turn,
        segment.reshape(slot_capacity, 1), segment.reshape(1, slot_capacity),
        token_position.reshape(1, slot_capacity),
    )


def normalize(rows, norm_gain):
    numbers = rows.astype(jnp.float32)
    factor = lax.rsqrt(jnp.mean(numbers * numbers, axis=-1, keepdims=True) + norm_eps)
    return (numbers * factor * norm_gain[None, :]).astype(jnp.bfloat16)


def project(attended_context, hidden_in, out_weight):
    return (
        hidden_in.astype(jnp.float32)
        + jnp.dot(attended_context, out_weight, preferred_element_type=jnp.float32)
    ).astype(jnp.bfloat16)


def feed_forward(normed, gate_weight, up_weight, down_weight):
    groups = lax.axis_size("grp")
    chunks = [normed]
    for k in range(1, groups):
        chunks.append(lax.ppermute(normed, "grp", [(j, (j + k) % groups) for j in range(groups)]))
    total = None
    for k, rows in enumerate(chunks):
        gate = jnp.dot(rows, gate_weight, preferred_element_type=jnp.float32)
        upward = jnp.dot(rows, up_weight, preferred_element_type=jnp.float32)
        hidden = (jax.nn.silu(gate) * upward).astype(jnp.bfloat16)
        part = jnp.dot(hidden, down_weight, preferred_element_type=jnp.float32).astype(jnp.bfloat16)
        if k:
            part = lax.ppermute(part, "grp", [(j, (j - k) % groups) for j in range(groups)])
        part = part.astype(jnp.float32)
        total = part if total is None else total + part
    return total


def on_device(
    hidden_in,
    queries,
    projected_keys,
    projected_values,
    segment,
    live_rows,
    out_weight,
    norm_gain,
    gate_weight,
    up_weight,
    down_weight,
):
    slot_capacity = hidden_in.shape[0]
    attended_context = attend(
        queries, projected_keys, projected_values, segment.reshape(slot_capacity)
    )
    slots = jnp.arange(slot_capacity, dtype=jnp.int32)
    own_count = live_rows.reshape(())
    request_owners = lax.axis_size("req")
    own_index = lax.axis_index("req")
    block_rows = slot_capacity // request_owners
    counts = lax.all_to_all(
        jnp.broadcast_to(live_rows.reshape(1, 1), (request_owners, LANES)), "req", 0, 0, tiled=True
    )[:, 0]
    ends = jnp.cumsum(counts)
    firsts = ends - counts
    owner_ids = jnp.arange(request_owners, dtype=jnp.int32)
    own_first = jnp.sum(jnp.where(owner_ids == own_index, firsts, 0))
    own_shift = own_first % request_owners
    keep = slots < own_count
    stream = jnp.arange(BAL, dtype=jnp.int32) * request_owners + own_index
    source = jnp.sum((ends[None, :] <= stream[:, None]).astype(jnp.int32), axis=1)
    source_first = jnp.sum(
        jnp.where(source[:, None] == owner_ids[None, :], firsts[None, :], 0), axis=1
    )
    pick = (stream - source_first) // request_owners * request_owners + source
    rows = project(attended_context, hidden_in, out_weight)
    kept = jnp.where(keep[:, None], rows, jnp.zeros_like(rows))
    arrived = lax.all_to_all(
        jnp.roll(kept.reshape(block_rows, request_owners, rows.shape[1]), own_shift, axis=1),
        "req",
        split_axis=1,
        concat_axis=1,
        tiled=True,
    )
    mixed = arrived.reshape(slot_capacity, -1)[pick]
    normed = normalize(mixed, norm_gain)
    result = (
        mixed.astype(jnp.float32) + feed_forward(normed, gate_weight, up_weight, down_weight)
    ).astype(jnp.bfloat16)
    lanes = (own_index - firsts) % request_owners
    source_row = jnp.arange(block_rows, dtype=jnp.int32)[:, None] * request_owners + lanes[None, :]
    valid = source_row < counts[None, :]
    target = jnp.where(valid, (firsts[None, :] + source_row) // request_owners, 0)
    outgoing = jnp.where(valid[:, :, None], result[target], jnp.zeros((), jnp.bfloat16))
    returned = lax.all_to_all(outgoing, "req", split_axis=1, concat_axis=1, tiled=True)
    return jnp.roll(returned, -own_shift, axis=1).reshape(slot_capacity, -1)


def solution(mesh):
    placed = (
        P(("req", "grp"), None),
        P(("req", "grp"), None),
        P(("req", "grp"), None),
        P(("req", "grp"), None),
        P("req", "grp", None),
        P("req", "grp"),
        P(),
        P(),
        P(None, "grp"),
        P(None, "grp"),
        P("grp", None),
    )
    return jax.shard_map(
        on_device, mesh=mesh, in_specs=placed, out_specs=P(("req", "grp"), None), check_vma=False
    )
```

```python
import math

import jax
import jax.numpy as jnp
from jax import lax
from jax.experimental import pallas as pl
from jax.experimental.pallas import tpu as pltpu
from jax.sharding import PartitionSpec as P

QUERY_HEADS = 20
KEY_VALUE_HEADS = 5
HEAD_SIZE = 64
WINDOW = 128
SINK = 4
BAL = 128


rope_base = 10000.0
norm_eps = 1e-05
LANES = 128


def rotation_tables(token_position):
    half = HEAD_SIZE // 2
    inverse = rope_base ** (-(2.0 * jnp.arange(half, dtype=jnp.float32)) / HEAD_SIZE)
    angle = token_position.astype(jnp.float32)[:, None] * inverse[None, :]
    reps = LANES // half
    return jnp.tile(jnp.cos(angle), (1, reps)), jnp.tile(jnp.sin(angle), (1, reps))


def half_turn_matrix():
    lane = jnp.arange(LANES, dtype=jnp.int32)
    local = lane % HEAD_SIZE
    half = HEAD_SIZE // 2
    src = jnp.where(local < half, lane + half, lane - half)
    sign = jnp.where(local < half, -1.0, 1.0)
    turn = jnp.where(lane[:, None] == src[None, :], sign[None, :], 0.0)
    return turn.astype(jnp.bfloat16)


def attention_kernel(q_ref, k_ref, v_ref, cos_ref, sin_ref, turn_ref, segc_ref, segr_ref, posr_ref, w_ref, h_ref, out_ref, bias_ref, acc_ref):
    slots = q_ref.shape[0]
    block = LANES

    @pl.when(pl.program_id(0) == 0)
    def _():
        qi = lax.broadcasted_iota(jnp.int32, (slots, slots), 0)
        ki = lax.broadcasted_iota(jnp.int32, (slots, slots), 1)
        allowed = (segc_ref[...] == segr_ref[...]) & (ki <= qi)
        allowed = allowed & ((qi - ki < WINDOW) | (posr_ref[...] < SINK))
        bias_ref[...] = jnp.where(allowed, 0.0, -jnp.inf).astype(jnp.float32)
        acc_ref[...] = h_ref[...].astype(jnp.float32)

    cosine = cos_ref[...]
    sine = sin_ref[...]
    turn = turn_ref[...]

    def rotate(x):
        turned = jnp.dot(x, turn, preferred_element_type=jnp.float32)
        return (x.astype(jnp.float32) * cosine + turned * sine).astype(jnp.bfloat16)

    q_rot = rotate(q_ref[...])
    k_rot = rotate(k_ref[...])
    v = v_ref[...]
    lane = lax.broadcasted_iota(jnp.int32, (1, LANES), 1)
    low = lane < HEAD_SIZE
    zero = jnp.zeros((), jnp.bfloat16)
    q_low = jnp.where(low, q_rot, zero)
    q_high = jnp.where(low, zero, q_rot)
    scale = 1.0 / math.sqrt(HEAD_SIZE)
    for i in range(slots // block):
        keys = block * (i + 1)
        k_part = k_rot[:keys]
        v_part = v[:keys]
        bias = bias_ref[i * block:(i + 1) * block, :keys]
        parts = []
        for qh in (q_low, q_high):
            scores = lax.dot_general(
                qh[i * block:(i + 1) * block], k_part, (((1,), (1,)), ((), ())),
                preferred_element_type=jnp.float32,
            )
            scores = scores * scale + bias
            largest = jnp.max(scores, axis=-1, keepdims=True)
            raised = jnp.exp(scores - largest)
            total = jnp.sum(raised, axis=-1, keepdims=True)
            weights = (raised * (1.0 / total)).astype(jnp.bfloat16)
            parts.append(jnp.dot(weights, v_part, preferred_element_type=jnp.float32))
        context = jnp.where(low, parts[0], parts[1]).astype(jnp.bfloat16)
        acc_ref[i * block:(i + 1) * block, :] += jnp.dot(
            context, w_ref[...], preferred_element_type=jnp.float32
        )

    @pl.when(pl.program_id(0) == pl.num_programs(0) - 1)
    def _():
        out_ref[...] = acc_ref[...].astype(out_ref.dtype)


def attend(queries, projected_keys, projected_values, segment, out_weight, hidden_in):
    slot_capacity = queries.shape[0]
    slots = jnp.arange(slot_capacity, dtype=jnp.int32)
    begins = jnp.concatenate([jnp.ones((1,), dtype=jnp.bool_), segment[1:] != segment[:-1]])
    starts = lax.cummax(jnp.where(begins, slots, 0), axis=0)
    token_position = slots - starts
    cosine, sine = rotation_tables(token_position)
    turn = half_turn_matrix()
    def doubled(x):
        x = x.reshape(slot_capacity, KEY_VALUE_HEADS, 1, HEAD_SIZE)
        x = jnp.broadcast_to(x, (slot_capacity, KEY_VALUE_HEADS, 2, HEAD_SIZE))
        return x.reshape(slot_capacity, KEY_VALUE_HEADS * 2 * HEAD_SIZE)
    keys2 = doubled(projected_keys)
    values2 = doubled(projected_values)
    tiles = QUERY_HEADS * HEAD_SIZE // LANES
    per_kv = tiles // KEY_VALUE_HEADS
    full = lambda t: (0, 0)
    width = out_weight.shape[1]
    return pl.pallas_call(
        attention_kernel,
        grid=(tiles,),
        in_specs=[
            pl.BlockSpec((slot_capacity, LANES), lambda t: (0, t)),
            pl.BlockSpec((slot_capacity, LANES), lambda t: (0, t // per_kv)),
            pl.BlockSpec((slot_capacity, LANES), lambda t: (0, t // per_kv)),
            pl.BlockSpec((slot_capacity, LANES), full),
            pl.BlockSpec((slot_capacity, LANES), full),
            pl.BlockSpec((LANES, LANES), full),
            pl.BlockSpec((slot_capacity, 1), full),
            pl.BlockSpec((1, slot_capacity), full),
            pl.BlockSpec((1, slot_capacity), full),
            pl.BlockSpec((LANES, width), lambda t: (t, 0)),
            pl.BlockSpec((slot_capacity, width), full),
        ],
        out_specs=pl.BlockSpec((slot_capacity, width), full),
        out_shape=jax.ShapeDtypeStruct((slot_capacity, width), jnp.bfloat16),
        scratch_shapes=[
            pltpu.VMEM((slot_capacity, slot_capacity), jnp.float32),
            pltpu.VMEM((slot_capacity, width), jnp.float32),
        ],
        compiler_params=pltpu.CompilerParams(dimension_semantics=("arbitrary",)),
    )(
        queries, keys2, values2, cosine, sine, turn,
        segment.reshape(slot_capacity, 1), segment.reshape(1, slot_capacity),
        token_position.reshape(1, slot_capacity), out_weight, hidden_in,
    )


def normalize(rows, norm_gain):
    numbers = rows.astype(jnp.float32)
    factor = lax.rsqrt(jnp.mean(numbers * numbers, axis=-1, keepdims=True) + norm_eps)
    return (numbers * factor * norm_gain[None, :]).astype(jnp.bfloat16)


def project(attended_context, hidden_in, out_weight):
    return (
        hidden_in.astype(jnp.float32)
        + jnp.dot(attended_context, out_weight, preferred_element_type=jnp.float32)
    ).astype(jnp.bfloat16)


def ffn_rows(rows, gate_weight, up_weight, down_weight):
    gate = jnp.dot(rows, gate_weight, preferred_element_type=jnp.float32)
    upward = jnp.dot(rows, up_weight, preferred_element_type=jnp.float32)
    hidden = (jax.nn.silu(gate) * upward).astype(jnp.bfloat16)
    return jnp.dot(hidden, down_weight, preferred_element_type=jnp.float32).astype(jnp.bfloat16)


def feed_forward(normed, gate_weight, up_weight, down_weight):
    groups = lax.axis_size("grp")
    rows = normed.shape[0]
    arrived = [
        lax.ppermute(normed, "grp", [(j, (j + k) % groups) for j in range(groups)])
        for k in range(1, groups)
    ]
    own = ffn_rows(normed, gate_weight, up_weight, down_weight)
    others = ffn_rows(jnp.concatenate(arrived, axis=0), gate_weight, up_weight, down_weight)
    total = own.astype(jnp.float32)
    for k in range(1, groups):
        part = others[(k - 1) * rows:k * rows]
        part = lax.ppermute(part, "grp", [(j, (j - k) % groups) for j in range(groups)])
        total = total + part.astype(jnp.float32)
    return total


def on_device(
    hidden_in,
    queries,
    projected_keys,
    projected_values,
    segment,
    live_rows,
    out_weight,
    norm_gain,
    gate_weight,
    up_weight,
    down_weight,
):
    slot_capacity = hidden_in.shape[0]
    rows = attend(
        queries, projected_keys, projected_values, segment.reshape(slot_capacity), out_weight, hidden_in
    )
    slots = jnp.arange(slot_capacity, dtype=jnp.int32)
    own_count = live_rows.reshape(())
    request_owners = lax.axis_size("req")
    own_index = lax.axis_index("req")
    block_rows = slot_capacity // request_owners
    counts = lax.all_to_all(
        jnp.broadcast_to(live_rows.reshape(1, 1), (request_owners, LANES)), "req", 0, 0, tiled=True
    )[:, 0]
    ends = jnp.cumsum(counts)
    firsts = ends - counts
    owner_ids = jnp.arange(request_owners, dtype=jnp.int32)
    own_first = jnp.sum(jnp.where(owner_ids == own_index, firsts, 0))
    own_shift = own_first % request_owners
    keep = slots < own_count
    stream = jnp.arange(BAL, dtype=jnp.int32) * request_owners + own_index
    source = jnp.sum((ends[None, :] <= stream[:, None]).astype(jnp.int32), axis=1)
    source_first = jnp.sum(
        jnp.where(source[:, None] == owner_ids[None, :], firsts[None, :], 0), axis=1
    )
    pick = (stream - source_first) // request_owners * request_owners + source
    kept = jnp.where(keep[:, None], rows, jnp.zeros_like(rows))
    arrived = lax.all_to_all(
        jnp.roll(kept.reshape(block_rows, request_owners, rows.shape[1]), own_shift, axis=1),
        "req",
        split_axis=1,
        concat_axis=1,
        tiled=True,
    )
    mixed = arrived.reshape(slot_capacity, -1)[pick]
    normed = normalize(mixed, norm_gain)
    result = (
        mixed.astype(jnp.float32) + feed_forward(normed, gate_weight, up_weight, down_weight)
    ).astype(jnp.bfloat16)
    lanes = (own_index - firsts) % request_owners
    source_row = jnp.arange(block_rows, dtype=jnp.int32)[:, None] * request_owners + lanes[None, :]
    valid = source_row < counts[None, :]
    target = jnp.where(valid, (firsts[None, :] + source_row) // request_owners, 0)
    outgoing = jnp.where(valid[:, :, None], result[target], jnp.zeros((), jnp.bfloat16))
    returned = lax.all_to_all(outgoing, "req", split_axis=1, concat_axis=1, tiled=True)
    return jnp.roll(returned, -own_shift, axis=1).reshape(slot_capacity, -1)


def solution(mesh):
    placed = (
        P(("req", "grp"), None),
        P(("req", "grp"), None),
        P(("req", "grp"), None),
        P(("req", "grp"), None),
        P("req", "grp", None),
        P("req", "grp"),
        P(),
        P(),
        P(None, "grp"),
        P(None, "grp"),
        P("grp", None),
    )
    return jax.shard_map(
        on_device, mesh=mesh, in_specs=placed, out_specs=P(("req", "grp"), None), check_vma=False
    )
```

```python
import math

import jax
import jax.numpy as jnp
from jax import lax
from jax.experimental import pallas as pl
from jax.experimental.pallas import tpu as pltpu
from jax.sharding import PartitionSpec as P

QUERY_HEADS = 20
KEY_VALUE_HEADS = 5
HEAD_SIZE = 64
WINDOW = 128
SINK = 4
BAL = 128


rope_base = 10000.0
norm_eps = 1e-05
LANES = 128


def rotation_tables(token_position):
    half = HEAD_SIZE // 2
    inverse = rope_base ** (-(2.0 * jnp.arange(half, dtype=jnp.float32)) / HEAD_SIZE)
    angle = token_position.astype(jnp.float32)[:, None] * inverse[None, :]
    reps = LANES // half
    return jnp.tile(jnp.cos(angle), (1, reps)), jnp.tile(jnp.sin(angle), (1, reps))


def half_turn_matrix():
    lane = jnp.arange(LANES, dtype=jnp.int32)
    local = lane % HEAD_SIZE
    half = HEAD_SIZE // 2
    src = jnp.where(local < half, lane + half, lane - half)
    sign = jnp.where(local < half, -1.0, 1.0)
    turn = jnp.where(lane[:, None] == src[None, :], sign[None, :], 0.0)
    return turn.astype(jnp.bfloat16)


def attention_kernel(q_ref, k_ref, v_ref, cos_ref, sin_ref, turn_ref, segc_ref, segr_ref, posr_ref, w_ref, h_ref, out_ref, bias_ref, acc_ref):
    slots = q_ref.shape[0]
    block = LANES

    @pl.when(pl.program_id(0) == 0)
    def _():
        qi = lax.broadcasted_iota(jnp.int32, (slots, slots), 0)
        ki = lax.broadcasted_iota(jnp.int32, (slots, slots), 1)
        allowed = (segc_ref[...] == segr_ref[...]) & (ki <= qi)
        allowed = allowed & ((qi - ki < WINDOW) | (posr_ref[...] < SINK))
        bias_ref[...] = jnp.where(allowed, 0.0, -jnp.inf).astype(jnp.float32)
        acc_ref[...] = h_ref[...].astype(jnp.float32)

    cosine = cos_ref[...]
    sine = sin_ref[...]
    turn = turn_ref[...]

    def rotate(x):
        turned = jnp.dot(x, turn, preferred_element_type=jnp.float32)
        return (x.astype(jnp.float32) * cosine + turned * sine).astype(jnp.bfloat16)

    q_rot = rotate(q_ref[...]) * jnp.bfloat16(1.0 / math.sqrt(HEAD_SIZE))
    k_rot = rotate(k_ref[...])
    v = v_ref[...]
    lane = lax.broadcasted_iota(jnp.int32, (1, LANES), 1)
    low = lane < HEAD_SIZE
    zero = jnp.zeros((), jnp.bfloat16)
    q_low = jnp.where(low, q_rot, zero)
    q_high = jnp.where(low, zero, q_rot)
    for i in range(slots // block):
        keys = block * (i + 1)
        k_part = k_rot[:keys]
        v_part = v[:keys]
        bias = bias_ref[i * block:(i + 1) * block, :keys]
        parts = []
        for qh in (q_low, q_high):
            scores = lax.dot_general(
                qh[i * block:(i + 1) * block], k_part, (((1,), (1,)), ((), ())),
                preferred_element_type=jnp.float32,
            )
            scores = scores + bias
            largest = jnp.max(scores, axis=-1, keepdims=True)
            raised = jnp.exp(scores - largest)
            total = jnp.sum(raised, axis=-1, keepdims=True)
            weights = (raised * (1.0 / total)).astype(jnp.bfloat16)
            parts.append(jnp.dot(weights, v_part, preferred_element_type=jnp.float32))
        context = jnp.where(low, parts[0], parts[1]).astype(jnp.bfloat16)
        acc_ref[i * block:(i + 1) * block, :] += jnp.dot(
            context, w_ref[...], preferred_element_type=jnp.float32
        )

    @pl.when(pl.program_id(0) == pl.num_programs(0) - 1)
    def _():
        out_ref[...] = acc_ref[...].astype(out_ref.dtype)


def attend(queries, projected_keys, projected_values, segment, out_weight, hidden_in):
    slot_capacity = queries.shape[0]
    slots = jnp.arange(slot_capacity, dtype=jnp.int32)
    begins = jnp.concatenate([jnp.ones((1,), dtype=jnp.bool_), segment[1:] != segment[:-1]])
    starts = lax.cummax(jnp.where(begins, slots, 0), axis=0)
    token_position = slots - starts
    cosine, sine = rotation_tables(token_position)
    turn = half_turn_matrix()
    def doubled(x):
        x = x.reshape(slot_capacity, KEY_VALUE_HEADS, 1, HEAD_SIZE)
        x = jnp.broadcast_to(x, (slot_capacity, KEY_VALUE_HEADS, 2, HEAD_SIZE))
        return x.reshape(slot_capacity, KEY_VALUE_HEADS * 2 * HEAD_SIZE)
    keys2 = doubled(projected_keys)
    values2 = doubled(projected_values)
    tiles = QUERY_HEADS * HEAD_SIZE // LANES
    per_kv = tiles // KEY_VALUE_HEADS
    full = lambda t: (0, 0)
    width = out_weight.shape[1]
    return pl.pallas_call(
        attention_kernel,
        grid=(tiles,),
        in_specs=[
            pl.BlockSpec((slot_capacity, LANES), lambda t: (0, t)),
            pl.BlockSpec((slot_capacity, LANES), lambda t: (0, t // per_kv)),
            pl.BlockSpec((slot_capacity, LANES), lambda t: (0, t // per_kv)),
            pl.BlockSpec((slot_capacity, LANES), full),
            pl.BlockSpec((slot_capacity, LANES), full),
            pl.BlockSpec((LANES, LANES), full),
            pl.BlockSpec((slot_capacity, 1), full),
            pl.BlockSpec((1, slot_capacity), full),
            pl.BlockSpec((1, slot_capacity), full),
            pl.BlockSpec((LANES, width), lambda t: (t, 0)),
            pl.BlockSpec((slot_capacity, width), full),
        ],
        out_specs=pl.BlockSpec((slot_capacity, width), full),
        out_shape=jax.ShapeDtypeStruct((slot_capacity, width), jnp.bfloat16),
        scratch_shapes=[
            pltpu.VMEM((slot_capacity, slot_capacity), jnp.float32),
            pltpu.VMEM((slot_capacity, width), jnp.float32),
        ],
        compiler_params=pltpu.CompilerParams(dimension_semantics=("arbitrary",)),
    )(
        queries, keys2, values2, cosine, sine, turn,
        segment.reshape(slot_capacity, 1), segment.reshape(1, slot_capacity),
        token_position.reshape(1, slot_capacity), out_weight, hidden_in,
    )


def normalize(rows, norm_gain):
    numbers = rows.astype(jnp.float32)
    factor = lax.rsqrt(jnp.mean(numbers * numbers, axis=-1, keepdims=True) + norm_eps)
    return (numbers * factor * norm_gain[None, :]).astype(jnp.bfloat16)


def project(attended_context, hidden_in, out_weight):
    return (
        hidden_in.astype(jnp.float32)
        + jnp.dot(attended_context, out_weight, preferred_element_type=jnp.float32)
    ).astype(jnp.bfloat16)


def ffn_rows(rows, gate_weight, up_weight, down_weight):
    gate = jnp.dot(rows, gate_weight, preferred_element_type=jnp.float32)
    upward = jnp.dot(rows, up_weight, preferred_element_type=jnp.float32)
    hidden = (jax.nn.silu(gate) * upward).astype(jnp.bfloat16)
    return jnp.dot(hidden, down_weight, preferred_element_type=jnp.float32).astype(jnp.bfloat16)


def feed_forward(normed, gate_weight, up_weight, down_weight):
    groups = lax.axis_size("grp")
    rows = normed.shape[0]
    arrived = [
        lax.ppermute(normed, "grp", [(j, (j + k) % groups) for j in range(groups)])
        for k in range(1, groups)
    ]
    own = ffn_rows(normed, gate_weight, up_weight, down_weight)
    own, *arrived = lax.optimization_barrier((own, *arrived))
    others = ffn_rows(jnp.concatenate(arrived, axis=0), gate_weight, up_weight, down_weight)
    total = own.astype(jnp.float32)
    for k in range(1, groups):
        part = others[(k - 1) * rows:k * rows]
        part = lax.ppermute(part, "grp", [(j, (j - k) % groups) for j in range(groups)])
        total = total + part.astype(jnp.float32)
    return total


def on_device(
    hidden_in,
    queries,
    projected_keys,
    projected_values,
    segment,
    live_rows,
    out_weight,
    norm_gain,
    gate_weight,
    up_weight,
    down_weight,
):
    slot_capacity = hidden_in.shape[0]
    rows = attend(
        queries, projected_keys, projected_values, segment.reshape(slot_capacity), out_weight, hidden_in
    )
    slots = jnp.arange(slot_capacity, dtype=jnp.int32)
    own_count = live_rows[lax.axis_index("req"), lax.axis_index("grp")]
    request_owners = lax.axis_size("req")
    own_index = lax.axis_index("req")
    block_rows = slot_capacity // request_owners
    counts = live_rows[:, lax.axis_index("grp")]
    ends = jnp.cumsum(counts)
    firsts = ends - counts
    owner_ids = jnp.arange(request_owners, dtype=jnp.int32)
    own_first = jnp.sum(jnp.where(owner_ids == own_index, firsts, 0))
    own_shift = own_first % request_owners
    keep = slots < own_count
    stream = jnp.arange(BAL, dtype=jnp.int32) * request_owners + own_index
    source = jnp.sum((ends[None, :] <= stream[:, None]).astype(jnp.int32), axis=1)
    source_first = jnp.sum(
        jnp.where(source[:, None] == owner_ids[None, :], firsts[None, :], 0), axis=1
    )
    pick = (stream - source_first) // request_owners * request_owners + source
    kept = jnp.where(keep[:, None], rows, jnp.zeros_like(rows))
    arrived = lax.all_to_all(
        jnp.roll(kept.reshape(block_rows, request_owners, rows.shape[1]), own_shift, axis=1),
        "req",
        split_axis=1,
        concat_axis=1,
        tiled=True,
    )
    mixed = arrived.reshape(slot_capacity, -1)[pick]
    normed = normalize(mixed, norm_gain)
    result = (
        mixed.astype(jnp.float32) + feed_forward(normed, gate_weight, up_weight, down_weight)
    ).astype(jnp.bfloat16)
    lanes = (own_index - firsts) % request_owners
    source_row = jnp.arange(block_rows, dtype=jnp.int32)[:, None] * request_owners + lanes[None, :]
    valid = source_row < counts[None, :]
    target = jnp.where(valid, (firsts[None, :] + source_row) // request_owners, 0)
    outgoing = jnp.where(valid[:, :, None], result[target], jnp.zeros((), jnp.bfloat16))
    returned = lax.all_to_all(outgoing, "req", split_axis=1, concat_axis=1, tiled=True)
    return jnp.roll(returned, -own_shift, axis=1).reshape(slot_capacity, -1)


def solution(mesh):
    placed = (
        P(("req", "grp"), None),
        P(("req", "grp"), None),
        P(("req", "grp"), None),
        P(("req", "grp"), None),
        P("req", "grp", None),
        P(),
        P(),
        P(),
        P(None, "grp"),
        P(None, "grp"),
        P("grp", None),
    )
    return jax.shard_map(
        on_device, mesh=mesh, in_specs=placed, out_specs=P(("req", "grp"), None), check_vma=False
    )
```

```python
import math

import jax
import jax.numpy as jnp
from jax import lax
from jax.experimental import pallas as pl
from jax.experimental.pallas import tpu as pltpu
from jax.sharding import PartitionSpec as P

QUERY_HEADS = 20
KEY_VALUE_HEADS = 5
HEAD_SIZE = 64
WINDOW = 128
SINK = 4
BAL = 128


rope_base = 10000.0
norm_eps = 1e-05
LANES = 128


def rotation_tables(token_position):
    half = HEAD_SIZE // 2
    inverse = rope_base ** (-(2.0 * jnp.arange(half, dtype=jnp.float32)) / HEAD_SIZE)
    angle = token_position.astype(jnp.float32)[:, None] * inverse[None, :]
    reps = LANES // half
    return jnp.tile(jnp.cos(angle), (1, reps)), jnp.tile(jnp.sin(angle), (1, reps))


def half_turn_matrix():
    lane = jnp.arange(LANES, dtype=jnp.int32)
    local = lane % HEAD_SIZE
    half = HEAD_SIZE // 2
    src = jnp.where(local < half, lane + half, lane - half)
    sign = jnp.where(local < half, -1.0, 1.0)
    turn = jnp.where(lane[:, None] == src[None, :], sign[None, :], 0.0)
    return turn.astype(jnp.bfloat16)


def attention_kernel(q_ref, k_ref, v_ref, cos_ref, sin_ref, turn_ref, segc_ref, segr_ref, posr_ref, w_ref, h_ref, out_ref, bias_ref, acc_ref):
    slots = q_ref.shape[0]
    block = LANES

    @pl.when(pl.program_id(0) == 0)
    def _():
        qi = lax.broadcasted_iota(jnp.int32, (slots, slots), 0)
        ki = lax.broadcasted_iota(jnp.int32, (slots, slots), 1)
        allowed = (segc_ref[...] == segr_ref[...]) & (ki <= qi)
        allowed = allowed & ((qi - ki < WINDOW) | (posr_ref[...] < SINK))
        bias_ref[...] = jnp.where(allowed, 0.0, -jnp.inf).astype(jnp.float32)
        acc_ref[...] = h_ref[...].astype(jnp.float32)

    cosine = cos_ref[...]
    sine = sin_ref[...]
    turn = turn_ref[...]

    def rotate(x):
        turned = jnp.dot(x, turn, preferred_element_type=jnp.float32)
        return (x.astype(jnp.float32) * cosine + turned * sine).astype(jnp.bfloat16)

    q_rot = rotate(q_ref[...]) * jnp.bfloat16(1.0 / math.sqrt(HEAD_SIZE))
    k_rot = rotate(k_ref[...])
    v = v_ref[...]
    lane = lax.broadcasted_iota(jnp.int32, (1, LANES), 1)
    low = lane < HEAD_SIZE
    zero = jnp.zeros((), jnp.bfloat16)
    q_low = jnp.where(low, q_rot, zero)
    q_high = jnp.where(low, zero, q_rot)
    for i in range(slots // block):
        keys = block * (i + 1)
        k_part = k_rot[:keys]
        v_part = v[:keys]
        bias = bias_ref[i * block:(i + 1) * block, :keys]
        parts = []
        for qh in (q_low, q_high):
            scores = lax.dot_general(
                qh[i * block:(i + 1) * block], k_part, (((1,), (1,)), ((), ())),
                preferred_element_type=jnp.float32,
            )
            scores = scores + bias
            largest = jnp.max(scores, axis=-1, keepdims=True)
            raised = jnp.exp(scores - largest)
            total = jnp.sum(raised, axis=-1, keepdims=True)
            weights = (raised * (1.0 / total)).astype(jnp.bfloat16)
            parts.append(jnp.dot(weights, v_part, preferred_element_type=jnp.float32))
        context = jnp.where(low, parts[0], parts[1]).astype(jnp.bfloat16)
        acc_ref[i * block:(i + 1) * block, :] += jnp.dot(
            context, w_ref[...], preferred_element_type=jnp.float32
        )

    @pl.when(pl.program_id(0) == pl.num_programs(0) - 1)
    def _():
        out_ref[...] = acc_ref[...].astype(out_ref.dtype)


def attend(queries, projected_keys, projected_values, segment, out_weight, hidden_in):
    slot_capacity = queries.shape[0]
    slots = jnp.arange(slot_capacity, dtype=jnp.int32)
    begins = jnp.concatenate([jnp.ones((1,), dtype=jnp.bool_), segment[1:] != segment[:-1]])
    starts = lax.cummax(jnp.where(begins, slots, 0), axis=0)
    token_position = slots - starts
    cosine, sine = rotation_tables(token_position)
    turn = half_turn_matrix()
    def doubled(x):
        x = x.reshape(slot_capacity, KEY_VALUE_HEADS, 1, HEAD_SIZE)
        x = jnp.broadcast_to(x, (slot_capacity, KEY_VALUE_HEADS, 2, HEAD_SIZE))
        return x.reshape(slot_capacity, KEY_VALUE_HEADS * 2 * HEAD_SIZE)
    keys2 = doubled(projected_keys)
    values2 = doubled(projected_values)
    tiles = QUERY_HEADS * HEAD_SIZE // LANES
    per_kv = tiles // KEY_VALUE_HEADS
    full = lambda t: (0, 0)
    width = out_weight.shape[1]
    return pl.pallas_call(
        attention_kernel,
        grid=(tiles,),
        in_specs=[
            pl.BlockSpec((slot_capacity, LANES), lambda t: (0, t)),
            pl.BlockSpec((slot_capacity, LANES), lambda t: (0, t // per_kv)),
            pl.BlockSpec((slot_capacity, LANES), lambda t: (0, t // per_kv)),
            pl.BlockSpec((slot_capacity, LANES), full),
            pl.BlockSpec((slot_capacity, LANES), full),
            pl.BlockSpec((LANES, LANES), full),
            pl.BlockSpec((slot_capacity, 1), full),
            pl.BlockSpec((1, slot_capacity), full),
            pl.BlockSpec((1, slot_capacity), full),
            pl.BlockSpec((LANES, width), lambda t: (t, 0)),
            pl.BlockSpec((slot_capacity, width), full),
        ],
        out_specs=pl.BlockSpec((slot_capacity, width), full),
        out_shape=jax.ShapeDtypeStruct((slot_capacity, width), jnp.bfloat16),
        scratch_shapes=[
            pltpu.VMEM((slot_capacity, slot_capacity), jnp.float32),
            pltpu.VMEM((slot_capacity, width), jnp.float32),
        ],
        compiler_params=pltpu.CompilerParams(dimension_semantics=("arbitrary",)),
    )(
        queries, keys2, values2, cosine, sine, turn,
        segment.reshape(slot_capacity, 1), segment.reshape(1, slot_capacity),
        token_position.reshape(1, slot_capacity), out_weight, hidden_in,
    )


def normalize(rows, norm_gain):
    numbers = rows.astype(jnp.float32)
    factor = lax.rsqrt(jnp.mean(numbers * numbers, axis=-1, keepdims=True) + norm_eps)
    return (numbers * factor * norm_gain[None, :]).astype(jnp.bfloat16)


def project(attended_context, hidden_in, out_weight):
    return (
        hidden_in.astype(jnp.float32)
        + jnp.dot(attended_context, out_weight, preferred_element_type=jnp.float32)
    ).astype(jnp.bfloat16)


def ffn_rows(rows, gate_weight, up_weight, down_weight):
    gate = jnp.dot(rows, gate_weight, preferred_element_type=jnp.float32)
    upward = jnp.dot(rows, up_weight, preferred_element_type=jnp.float32)
    hidden = (jax.nn.silu(gate) * upward).astype(jnp.bfloat16)
    return jnp.dot(hidden, down_weight, preferred_element_type=jnp.float32).astype(jnp.bfloat16)


def feed_forward(normed, gate_weight, up_weight, down_weight):
    groups = lax.axis_size("grp")
    rows = normed.shape[0]
    arrived = [
        lax.ppermute(normed, "grp", [(j, (j + k) % groups) for j in range(groups)])
        for k in range(1, groups)
    ]
    own = ffn_rows(normed, gate_weight, up_weight, down_weight)
    own, *arrived = lax.optimization_barrier((own, *arrived))
    others = ffn_rows(jnp.concatenate(arrived, axis=0), gate_weight, up_weight, down_weight)
    total = own.astype(jnp.float32)
    for k in range(1, groups):
        part = others[(k - 1) * rows:k * rows]
        part = lax.ppermute(part, "grp", [(j, (j - k) % groups) for j in range(groups)])
        total = total + part.astype(jnp.float32)
    return total


def on_device(
    hidden_in,
    queries,
    projected_keys,
    projected_values,
    segment,
    live_rows,
    out_weight,
    norm_gain,
    gate_weight,
    up_weight,
    down_weight,
):
    slot_capacity = hidden_in.shape[0]
    rows = attend(
        queries, projected_keys, projected_values, segment.reshape(slot_capacity), out_weight, hidden_in
    )
    slots = jnp.arange(slot_capacity, dtype=jnp.int32)
    own_count = live_rows.reshape(())
    request_owners = lax.axis_size("req")
    own_index = lax.axis_index("req")
    block_rows = slot_capacity // request_owners
    counts = lax.all_to_all(
        jnp.broadcast_to(live_rows.reshape(1, 1), (request_owners, LANES)), "req", 0, 0, tiled=True
    )[:, 0]
    ends = jnp.cumsum(counts)
    firsts = ends - counts
    owner_ids = jnp.arange(request_owners, dtype=jnp.int32)
    own_first = jnp.sum(jnp.where(owner_ids == own_index, firsts, 0))
    own_shift = own_first % request_owners
    keep = slots < own_count
    stream = jnp.arange(BAL, dtype=jnp.int32) * request_owners + own_index
    source = jnp.sum((ends[None, :] <= stream[:, None]).astype(jnp.int32), axis=1)
    source_first = jnp.sum(
        jnp.where(source[:, None] == owner_ids[None, :], firsts[None, :], 0), axis=1
    )
    pick = (stream - source_first) // request_owners * request_owners + source
    kept = jnp.where(keep[:, None], rows, jnp.zeros_like(rows))
    arrived = lax.all_to_all(
        jnp.roll(kept.reshape(block_rows, request_owners, rows.shape[1]), own_shift, axis=1),
        "req",
        split_axis=1,
        concat_axis=1,
        tiled=True,
    )
    mixed = arrived.reshape(slot_capacity, -1)[pick]
    normed = normalize(mixed, norm_gain)
    result = (
        mixed.astype(jnp.float32) + feed_forward(normed, gate_weight, up_weight, down_weight)
    ).astype(jnp.bfloat16)
    lanes = (own_index - firsts) % request_owners
    source_row = jnp.arange(block_rows, dtype=jnp.int32)[:, None] * request_owners + lanes[None, :]
    valid = source_row < counts[None, :]
    target = jnp.where(valid, (firsts[None, :] + source_row) // request_owners, 0)
    outgoing = jnp.where(valid[:, :, None], result[target], jnp.zeros((), jnp.bfloat16))
    returned = lax.all_to_all(outgoing, "req", split_axis=1, concat_axis=1, tiled=True)
    return jnp.roll(returned, -own_shift, axis=1).reshape(slot_capacity, -1)


def solution(mesh):
    placed = (
        P(("req", "grp"), None),
        P(("req", "grp"), None),
        P(("req", "grp"), None),
        P(("req", "grp"), None),
        P("req", "grp", None),
        P("req", "grp"),
        P(),
        P(),
        P(None, "grp"),
        P(None, "grp"),
        P("grp", None),
    )
    return jax.shard_map(
        on_device, mesh=mesh, in_specs=placed, out_specs=P(("req", "grp"), None), check_vma=False
    )
```

```python
import math

import jax
import jax.numpy as jnp
from jax import lax
from jax.experimental import pallas as pl
from jax.experimental.pallas import tpu as pltpu
from jax.sharding import PartitionSpec as P

QUERY_HEADS = 20
KEY_VALUE_HEADS = 5
HEAD_SIZE = 64
WINDOW = 128
SINK = 4
BAL = 128


rope_base = 10000.0
norm_eps = 1e-05
LANES = 128


def rotation_tables(token_position):
    half = HEAD_SIZE // 2
    inverse = rope_base ** (-(2.0 * jnp.arange(half, dtype=jnp.float32)) / HEAD_SIZE)
    angle = token_position.astype(jnp.float32)[:, None] * inverse[None, :]
    reps = LANES // half
    return jnp.tile(jnp.cos(angle), (1, reps)), jnp.tile(jnp.sin(angle), (1, reps))


def half_turn_matrix():
    lane = jnp.arange(LANES, dtype=jnp.int32)
    local = lane % HEAD_SIZE
    half = HEAD_SIZE // 2
    src = jnp.where(local < half, lane + half, lane - half)
    sign = jnp.where(local < half, -1.0, 1.0)
    turn = jnp.where(lane[:, None] == src[None, :], sign[None, :], 0.0)
    return turn.astype(jnp.bfloat16)


def attention_kernel(q_ref, k_ref, v_ref, cos_ref, sin_ref, turn_ref, segc_ref, segr_ref, posr_ref, w_ref, h_ref, out_ref, bias_ref, acc_ref):
    slots = q_ref.shape[0]
    block = LANES

    @pl.when(pl.program_id(0) == 0)
    def _():
        qi = lax.broadcasted_iota(jnp.int32, (slots, slots), 0)
        ki = lax.broadcasted_iota(jnp.int32, (slots, slots), 1)
        allowed = (segc_ref[...] == segr_ref[...]) & (ki <= qi)
        allowed = allowed & ((qi - ki < WINDOW) | (posr_ref[...] < SINK))
        bias_ref[...] = jnp.where(allowed, 0.0, -jnp.inf).astype(jnp.float32)
        acc_ref[...] = h_ref[...].astype(jnp.float32)

    cosine = cos_ref[...]
    sine = sin_ref[...]
    turn = turn_ref[...]

    def rotate(x):
        turned = jnp.dot(x, turn, preferred_element_type=jnp.float32)
        return (x.astype(jnp.float32) * cosine + turned * sine).astype(jnp.bfloat16)

    q_rot = rotate(q_ref[...]) * jnp.bfloat16(1.0 / math.sqrt(HEAD_SIZE))
    k_rot = rotate(k_ref[...])
    v = v_ref[...]
    lane = lax.broadcasted_iota(jnp.int32, (1, LANES), 1)
    low = lane < HEAD_SIZE
    zero = jnp.zeros((), jnp.bfloat16)
    q_low = jnp.where(low, q_rot, zero)
    q_high = jnp.where(low, zero, q_rot)
    for i in range(slots // block):
        keys = block * (i + 1)
        k_part = k_rot[:keys]
        v_part = v[:keys]
        bias = bias_ref[i * block:(i + 1) * block, :keys]
        parts = []
        for qh in (q_low, q_high):
            scores = lax.dot_general(
                qh[i * block:(i + 1) * block], k_part, (((1,), (1,)), ((), ())),
                preferred_element_type=jnp.float32,
            )
            scores = scores + bias
            largest = jnp.max(scores, axis=-1, keepdims=True)
            raised = jnp.exp(scores - largest)
            total = jnp.sum(raised, axis=-1, keepdims=True)
            weights = (raised * (1.0 / total)).astype(jnp.bfloat16)
            parts.append(jnp.dot(weights, v_part, preferred_element_type=jnp.float32))
        context = jnp.where(low, parts[0], parts[1]).astype(jnp.bfloat16)
        acc_ref[i * block:(i + 1) * block, :] += jnp.dot(
            context, w_ref[...], preferred_element_type=jnp.float32
        )

    @pl.when(pl.program_id(0) == pl.num_programs(0) - 1)
    def _():
        out_ref[...] = acc_ref[...].astype(out_ref.dtype)


def attend(queries, projected_keys, projected_values, segment, out_weight, hidden_in):
    slot_capacity = queries.shape[0]
    slots = jnp.arange(slot_capacity, dtype=jnp.int32)
    begins = jnp.concatenate([jnp.ones((1,), dtype=jnp.bool_), segment[1:] != segment[:-1]])
    starts = lax.cummax(jnp.where(begins, slots, 0), axis=0)
    token_position = slots - starts
    cosine, sine = rotation_tables(token_position)
    turn = half_turn_matrix()
    def doubled(x):
        x = x.reshape(slot_capacity, KEY_VALUE_HEADS, 1, HEAD_SIZE)
        x = jnp.broadcast_to(x, (slot_capacity, KEY_VALUE_HEADS, 2, HEAD_SIZE))
        return x.reshape(slot_capacity, KEY_VALUE_HEADS * 2 * HEAD_SIZE)
    keys2 = doubled(projected_keys)
    values2 = doubled(projected_values)
    tiles = QUERY_HEADS * HEAD_SIZE // LANES
    per_kv = tiles // KEY_VALUE_HEADS
    full = lambda t: (0, 0)
    width = out_weight.shape[1]
    return pl.pallas_call(
        attention_kernel,
        grid=(tiles,),
        in_specs=[
            pl.BlockSpec((slot_capacity, LANES), lambda t: (0, t)),
            pl.BlockSpec((slot_capacity, LANES), lambda t: (0, t // per_kv)),
            pl.BlockSpec((slot_capacity, LANES), lambda t: (0, t // per_kv)),
            pl.BlockSpec((slot_capacity, LANES), full),
            pl.BlockSpec((slot_capacity, LANES), full),
            pl.BlockSpec((LANES, LANES), full),
            pl.BlockSpec((slot_capacity, 1), full),
            pl.BlockSpec((1, slot_capacity), full),
            pl.BlockSpec((1, slot_capacity), full),
            pl.BlockSpec((LANES, width), lambda t: (t, 0)),
            pl.BlockSpec((slot_capacity, width), full),
        ],
        out_specs=pl.BlockSpec((slot_capacity, width), full),
        out_shape=jax.ShapeDtypeStruct((slot_capacity, width), jnp.bfloat16),
        scratch_shapes=[
            pltpu.VMEM((slot_capacity, slot_capacity), jnp.float32),
            pltpu.VMEM((slot_capacity, width), jnp.float32),
        ],
        compiler_params=pltpu.CompilerParams(dimension_semantics=("arbitrary",)),
    )(
        queries, keys2, values2, cosine, sine, turn,
        segment.reshape(slot_capacity, 1), segment.reshape(1, slot_capacity),
        token_position.reshape(1, slot_capacity), out_weight, hidden_in,
    )


def normalize(rows, norm_gain):
    numbers = rows.astype(jnp.float32)
    factor = lax.rsqrt(jnp.mean(numbers * numbers, axis=-1, keepdims=True) + norm_eps)
    return (numbers * factor * norm_gain[None, :]).astype(jnp.bfloat16)


def project(attended_context, hidden_in, out_weight):
    return (
        hidden_in.astype(jnp.float32)
        + jnp.dot(attended_context, out_weight, preferred_element_type=jnp.float32)
    ).astype(jnp.bfloat16)


def ffn_rows(rows, gate_weight, up_weight, down_weight):
    gate = jnp.dot(rows, gate_weight, preferred_element_type=jnp.float32)
    upward = jnp.dot(rows, up_weight, preferred_element_type=jnp.float32)
    hidden = (jax.nn.silu(gate) * upward).astype(jnp.bfloat16)
    return jnp.dot(hidden, down_weight, preferred_element_type=jnp.float32).astype(jnp.bfloat16)


def feed_forward(normed, gate_weight, up_weight, down_weight):
    groups = lax.axis_size("grp")
    rows = normed.shape[0]
    arrived = [
        lax.ppermute(normed, "grp", [(j, (j + k) % groups) for j in range(groups)])
        for k in range(1, groups)
    ]
    own = ffn_rows(normed, gate_weight, up_weight, down_weight)
    own, *arrived = lax.optimization_barrier((own, *arrived))
    others = ffn_rows(jnp.concatenate(arrived, axis=0), gate_weight, up_weight, down_weight)
    total = own.astype(jnp.float32)
    for k in range(1, groups):
        part = others[(k - 1) * rows:k * rows]
        part = lax.ppermute(part, "grp", [(j, (j - k) % groups) for j in range(groups)])
        total = total + part.astype(jnp.float32)
    return total


def on_device(
    hidden_in,
    queries,
    projected_keys,
    projected_values,
    segment,
    live_rows,
    out_weight,
    norm_gain,
    gate_weight,
    up_weight,
    down_weight,
):
    slot_capacity = hidden_in.shape[0]
    rows = attend(
        queries, projected_keys, projected_values, segment.reshape(slot_capacity), out_weight, hidden_in
    )
    slots = jnp.arange(slot_capacity, dtype=jnp.int32)
    own_count = live_rows.reshape(())
    request_owners = lax.axis_size("req")
    own_index = lax.axis_index("req")
    block_rows = slot_capacity // request_owners
    counts = lax.all_to_all(
        jnp.broadcast_to(live_rows.reshape(1, 1), (request_owners, LANES)), "req", 0, 0, tiled=True
    )[:, 0]
    ends = jnp.cumsum(counts)
    firsts = ends - counts
    owner_ids = jnp.arange(request_owners, dtype=jnp.int32)
    own_first = jnp.sum(jnp.where(owner_ids == own_index, firsts, 0))
    own_shift = own_first % request_owners
    stream = jnp.arange(BAL, dtype=jnp.int32) * request_owners + own_index
    source = jnp.sum((ends[None, :] <= stream[:, None]).astype(jnp.int32), axis=1)
    source_first = jnp.sum(
        jnp.where(source[:, None] == owner_ids[None, :], firsts[None, :], 0), axis=1
    )
    pick = source * block_rows + (stream - source_first) // request_owners
    dest = jnp.arange(request_owners, dtype=jnp.int32)[:, None]
    blocks = jnp.arange(block_rows, dtype=jnp.int32)[None, :]
    send_row = blocks * request_owners + (dest - own_shift) % request_owners
    outbound = jnp.where((send_row < own_count)[:, :, None], rows[send_row], jnp.zeros((), rows.dtype))
    arrived = lax.all_to_all(outbound, "req", 0, 0, tiled=True)
    mixed = arrived.reshape(slot_capacity, -1)[pick]
    normed = normalize(mixed, norm_gain)
    result = (
        mixed.astype(jnp.float32) + feed_forward(normed, gate_weight, up_weight, down_weight)
    ).astype(jnp.bfloat16)
    lanes = (own_index - firsts) % request_owners
    source_row = jnp.arange(block_rows, dtype=jnp.int32)[:, None] * request_owners + lanes[None, :]
    valid = source_row < counts[None, :]
    target = jnp.where(valid, (firsts[None, :] + source_row) // request_owners, 0)
    outgoing = jnp.where(valid.T[:, :, None], result[target.T], jnp.zeros((), jnp.bfloat16))
    returned = lax.all_to_all(outgoing, "req", 0, 0, tiled=True).reshape(slot_capacity, -1)
    back_row = ((slots % request_owners + own_shift) % request_owners) * block_rows + slots // request_owners
    return returned[back_row]


def solution(mesh):
    placed = (
        P(("req", "grp"), None),
        P(("req", "grp"), None),
        P(("req", "grp"), None),
        P(("req", "grp"), None),
        P("req", "grp", None),
        P("req", "grp"),
        P(),
        P(),
        P(None, "grp"),
        P(None, "grp"),
        P("grp", None),
    )
    return jax.shard_map(
        on_device, mesh=mesh, in_specs=placed, out_specs=P(("req", "grp"), None), check_vma=False
    )
```

```python
import math

import jax
import jax.numpy as jnp
from jax import lax
from jax.experimental import pallas as pl
from jax.experimental.pallas import tpu as pltpu
from jax.sharding import PartitionSpec as P

QUERY_HEADS = 20
KEY_VALUE_HEADS = 5
HEAD_SIZE = 64
WINDOW = 128
SINK = 4
BAL = 128


rope_base = 10000.0
norm_eps = 1e-05
LANES = 128


def rotation_tables(token_position):
    half = HEAD_SIZE // 2
    inverse = rope_base ** (-(2.0 * jnp.arange(half, dtype=jnp.float32)) / HEAD_SIZE)
    angle = token_position.astype(jnp.float32)[:, None] * inverse[None, :]
    reps = LANES // half
    return jnp.tile(jnp.cos(angle), (1, reps)), jnp.tile(jnp.sin(angle), (1, reps))


def half_turn_matrix():
    lane = jnp.arange(LANES, dtype=jnp.int32)
    local = lane % HEAD_SIZE
    half = HEAD_SIZE // 2
    src = jnp.where(local < half, lane + half, lane - half)
    sign = jnp.where(local < half, -1.0, 1.0)
    turn = jnp.where(lane[:, None] == src[None, :], sign[None, :], 0.0)
    return turn.astype(jnp.bfloat16)


def attention_kernel(q_ref, k_ref, v_ref, cos_ref, sin_ref, turn_ref, segc_ref, segr_ref, posr_ref, w_ref, h_ref, out_ref, bias_ref, acc_ref):
    slots = q_ref.shape[0]
    block = LANES

    @pl.when(pl.program_id(0) == 0)
    def _():
        qi = lax.broadcasted_iota(jnp.int32, (slots, slots), 0)
        ki = lax.broadcasted_iota(jnp.int32, (slots, slots), 1)
        allowed = (segc_ref[...] == segr_ref[...]) & (ki <= qi)
        allowed = allowed & ((qi - ki < WINDOW) | (posr_ref[...] < SINK))
        bias_ref[...] = jnp.where(allowed, 0.0, -jnp.inf).astype(jnp.float32)
        acc_ref[...] = h_ref[...].astype(jnp.float32)

    cosine = cos_ref[...]
    sine = sin_ref[...]
    turn = turn_ref[...]

    def rotate(x):
        turned = jnp.dot(x, turn, preferred_element_type=jnp.float32)
        return (x.astype(jnp.float32) * cosine + turned * sine).astype(jnp.bfloat16)

    q_rot = rotate(q_ref[...]) * jnp.bfloat16(1.0 / math.sqrt(HEAD_SIZE))
    k_rot = rotate(k_ref[...])
    v = v_ref[...]
    lane = lax.broadcasted_iota(jnp.int32, (1, LANES), 1)
    low = lane < HEAD_SIZE
    zero = jnp.zeros((), jnp.bfloat16)
    q_low = jnp.where(low, q_rot, zero)
    q_high = jnp.where(low, zero, q_rot)
    for i in range(slots // block):
        keys = block * (i + 1)
        k_part = k_rot[:keys]
        v_part = v[:keys]
        bias = bias_ref[i * block:(i + 1) * block, :keys]
        parts = []
        for qh in (q_low, q_high):
            scores = lax.dot_general(
                qh[i * block:(i + 1) * block], k_part, (((1,), (1,)), ((), ())),
                preferred_element_type=jnp.float32,
            )
            scores = scores + bias
            largest = jnp.max(scores, axis=-1, keepdims=True)
            raised = jnp.exp(scores - largest)
            total = jnp.sum(raised, axis=-1, keepdims=True)
            weights = (raised * (1.0 / total)).astype(jnp.bfloat16)
            parts.append(jnp.dot(weights, v_part, preferred_element_type=jnp.float32))
        context = jnp.where(low, parts[0], parts[1]).astype(jnp.bfloat16)
        acc_ref[i * block:(i + 1) * block, :] += jnp.dot(
            context, w_ref[...], preferred_element_type=jnp.float32
        )

    @pl.when(pl.program_id(0) == pl.num_programs(0) - 1)
    def _():
        out_ref[...] = acc_ref[...].astype(out_ref.dtype)


def attend(queries, projected_keys, projected_values, segment, out_weight, hidden_in):
    slot_capacity = queries.shape[0]
    slots = jnp.arange(slot_capacity, dtype=jnp.int32)
    begins = jnp.concatenate([jnp.ones((1,), dtype=jnp.bool_), segment[1:] != segment[:-1]])
    starts = lax.cummax(jnp.where(begins, slots, 0), axis=0)
    token_position = slots - starts
    cosine, sine = rotation_tables(token_position)
    turn = half_turn_matrix()
    def doubled(x):
        x = x.reshape(slot_capacity, KEY_VALUE_HEADS, 1, HEAD_SIZE)
        x = jnp.broadcast_to(x, (slot_capacity, KEY_VALUE_HEADS, 2, HEAD_SIZE))
        return x.reshape(slot_capacity, KEY_VALUE_HEADS * 2 * HEAD_SIZE)
    keys2 = doubled(projected_keys)
    values2 = doubled(projected_values)
    tiles = QUERY_HEADS * HEAD_SIZE // LANES
    per_kv = tiles // KEY_VALUE_HEADS
    full = lambda t: (0, 0)
    width = out_weight.shape[1]
    return pl.pallas_call(
        attention_kernel,
        grid=(tiles,),
        in_specs=[
            pl.BlockSpec((slot_capacity, LANES), lambda t: (0, t)),
            pl.BlockSpec((slot_capacity, LANES), lambda t: (0, t // per_kv)),
            pl.BlockSpec((slot_capacity, LANES), lambda t: (0, t // per_kv)),
            pl.BlockSpec((slot_capacity, LANES), full),
            pl.BlockSpec((slot_capacity, LANES), full),
            pl.BlockSpec((LANES, LANES), full),
            pl.BlockSpec((slot_capacity, 1), full),
            pl.BlockSpec((1, slot_capacity), full),
            pl.BlockSpec((1, slot_capacity), full),
            pl.BlockSpec((LANES, width), lambda t: (t, 0)),
            pl.BlockSpec((slot_capacity, width), full),
        ],
        out_specs=pl.BlockSpec((slot_capacity, width), full),
        out_shape=jax.ShapeDtypeStruct((slot_capacity, width), jnp.bfloat16),
        scratch_shapes=[
            pltpu.VMEM((slot_capacity, slot_capacity), jnp.float32),
            pltpu.VMEM((slot_capacity, width), jnp.float32),
        ],
        compiler_params=pltpu.CompilerParams(dimension_semantics=("arbitrary",)),
    )(
        queries, keys2, values2, cosine, sine, turn,
        segment.reshape(slot_capacity, 1), segment.reshape(1, slot_capacity),
        token_position.reshape(1, slot_capacity), out_weight, hidden_in,
    )


def normalize(rows, norm_gain):
    numbers = rows.astype(jnp.float32)
    factor = lax.rsqrt(jnp.mean(numbers * numbers, axis=-1, keepdims=True) + norm_eps)
    return (numbers * factor * norm_gain[None, :]).astype(jnp.bfloat16)


def project(attended_context, hidden_in, out_weight):
    return (
        hidden_in.astype(jnp.float32)
        + jnp.dot(attended_context, out_weight, preferred_element_type=jnp.float32)
    ).astype(jnp.bfloat16)


def ffn_rows(rows, gate_weight, up_weight, down_weight):
    gate = jnp.dot(rows, gate_weight, preferred_element_type=jnp.float32)
    upward = jnp.dot(rows, up_weight, preferred_element_type=jnp.float32)
    hidden = (jax.nn.silu(gate) * upward).astype(jnp.bfloat16)
    return jnp.dot(hidden, down_weight, preferred_element_type=jnp.float32).astype(jnp.bfloat16)


def feed_forward(normed, gate_weight, up_weight, down_weight):
    groups = lax.axis_size("grp")
    rows = normed.shape[0]
    arrived = [
        lax.ppermute(normed, "grp", [(j, (j + k) % groups) for j in range(groups)])
        for k in range(1, groups)
    ]
    own = ffn_rows(normed, gate_weight, up_weight, down_weight)
    own, *arrived = lax.optimization_barrier((own, *arrived))
    others = ffn_rows(jnp.concatenate(arrived, axis=0), gate_weight, up_weight, down_weight)
    total = own.astype(jnp.float32)
    for k in range(1, groups):
        part = others[(k - 1) * rows:k * rows]
        part = lax.ppermute(part, "grp", [(j, (j - k) % groups) for j in range(groups)])
        total = total + part.astype(jnp.float32)
    return total


def take_rows(table, index, valid):
    columns = jnp.arange(table.shape[0], dtype=jnp.int32)
    chosen = (index[:, None] == columns[None, :]) & valid[:, None]
    return jnp.dot(
        chosen.astype(table.dtype), table, preferred_element_type=jnp.float32
    ).astype(table.dtype)


def on_device(
    hidden_in,
    queries,
    projected_keys,
    projected_values,
    segment,
    live_rows,
    out_weight,
    norm_gain,
    gate_weight,
    up_weight,
    down_weight,
):
    slot_capacity = hidden_in.shape[0]
    rows = attend(
        queries, projected_keys, projected_values, segment.reshape(slot_capacity), out_weight, hidden_in
    )
    slots = jnp.arange(slot_capacity, dtype=jnp.int32)
    own_count = live_rows.reshape(())
    request_owners = lax.axis_size("req")
    own_index = lax.axis_index("req")
    block_rows = slot_capacity // request_owners
    counts = lax.all_to_all(
        jnp.broadcast_to(live_rows.reshape(1, 1), (request_owners, LANES)), "req", 0, 0, tiled=True
    )[:, 0]
    ends = jnp.cumsum(counts)
    firsts = ends - counts
    owner_ids = jnp.arange(request_owners, dtype=jnp.int32)
    own_first = jnp.sum(jnp.where(owner_ids == own_index, firsts, 0))
    own_shift = own_first % request_owners
    stream = jnp.arange(BAL, dtype=jnp.int32) * request_owners + own_index
    source = jnp.sum((ends[None, :] <= stream[:, None]).astype(jnp.int32), axis=1)
    source_first = jnp.sum(
        jnp.where(source[:, None] == owner_ids[None, :], firsts[None, :], 0), axis=1
    )
    pick = source * block_rows + (stream - source_first) // request_owners
    dest = jnp.arange(request_owners, dtype=jnp.int32)[:, None]
    blocks = jnp.arange(block_rows, dtype=jnp.int32)[None, :]
    send_row = blocks * request_owners + (dest - own_shift) % request_owners
    send_row = send_row.reshape(slot_capacity)
    outbound = take_rows(rows, send_row, send_row < own_count)
    arrived = lax.all_to_all(
        outbound.reshape(request_owners, block_rows, -1), "req", 0, 0, tiled=True
    )
    mixed = take_rows(arrived.reshape(slot_capacity, -1), pick, pick >= 0)
    normed = normalize(mixed, norm_gain)
    result = (
        mixed.astype(jnp.float32) + feed_forward(normed, gate_weight, up_weight, down_weight)
    ).astype(jnp.bfloat16)
    lanes = (own_index - firsts) % request_owners
    source_row = jnp.arange(block_rows, dtype=jnp.int32)[:, None] * request_owners + lanes[None, :]
    valid = source_row < counts[None, :]
    target = jnp.where(valid, (firsts[None, :] + source_row) // request_owners, 0)
    outgoing = take_rows(result, target.T.reshape(slot_capacity), valid.T.reshape(slot_capacity))
    returned = lax.all_to_all(
        outgoing.reshape(request_owners, block_rows, -1), "req", 0, 0, tiled=True
    ).reshape(slot_capacity, -1)
    back_row = ((slots % request_owners + own_shift) % request_owners) * block_rows + slots // request_owners
    return take_rows(returned, back_row, back_row >= 0)


def solution(mesh):
    placed = (
        P(("req", "grp"), None),
        P(("req", "grp"), None),
        P(("req", "grp"), None),
        P(("req", "grp"), None),
        P("req", "grp", None),
        P("req", "grp"),
        P(),
        P(),
        P(None, "grp"),
        P(None, "grp"),
        P("grp", None),
    )
    return jax.shard_map(
        on_device, mesh=mesh, in_specs=placed, out_specs=P(("req", "grp"), None), check_vma=False
    )
```

```python
import math

import jax
import jax.numpy as jnp
from jax import lax
from jax.experimental import pallas as pl
from jax.experimental.pallas import tpu as pltpu
from jax.sharding import PartitionSpec as P

QUERY_HEADS = 20
KEY_VALUE_HEADS = 5
HEAD_SIZE = 64
WINDOW = 128
SINK = 4
BAL = 128


rope_base = 10000.0
norm_eps = 1e-05
LANES = 128


def rotation_tables(token_position):
    half = HEAD_SIZE // 2
    inverse = rope_base ** (-(2.0 * jnp.arange(half, dtype=jnp.float32)) / HEAD_SIZE)
    angle = token_position.astype(jnp.float32)[:, None] * inverse[None, :]
    reps = LANES // half
    return jnp.tile(jnp.cos(angle), (1, reps)), jnp.tile(jnp.sin(angle), (1, reps))


def half_turn_matrix():
    lane = jnp.arange(LANES, dtype=jnp.int32)
    local = lane % HEAD_SIZE
    half = HEAD_SIZE // 2
    src = jnp.where(local < half, lane + half, lane - half)
    sign = jnp.where(local < half, -1.0, 1.0)
    turn = jnp.where(lane[:, None] == src[None, :], sign[None, :], 0.0)
    return turn.astype(jnp.bfloat16)


def attention_kernel(q_ref, k_ref, v_ref, cos_ref, sin_ref, turn_ref, segc_ref, segr_ref, posr_ref, w_ref, h_ref, out_ref, bias_ref, acc_ref):
    slots = q_ref.shape[0]
    block = LANES

    @pl.when(pl.program_id(0) == 0)
    def _():
        qi = lax.broadcasted_iota(jnp.int32, (slots, slots), 0)
        ki = lax.broadcasted_iota(jnp.int32, (slots, slots), 1)
        allowed = (segc_ref[...] == segr_ref[...]) & (ki <= qi)
        allowed = allowed & ((qi - ki < WINDOW) | (posr_ref[...] < SINK))
        bias_ref[...] = jnp.where(allowed, 0.0, -jnp.inf).astype(jnp.float32)
        acc_ref[...] = h_ref[...].astype(jnp.float32)

    cosine = cos_ref[...]
    sine = sin_ref[...]
    turn = turn_ref[...]

    def rotate(x):
        turned = jnp.dot(x, turn, preferred_element_type=jnp.float32)
        return (x.astype(jnp.float32) * cosine + turned * sine).astype(jnp.bfloat16)

    q_rot = rotate(q_ref[...]) * jnp.bfloat16(1.0 / math.sqrt(HEAD_SIZE))
    k_rot = rotate(k_ref[...])
    v = v_ref[...]
    lane = lax.broadcasted_iota(jnp.int32, (1, LANES), 1)
    low = lane < HEAD_SIZE
    zero = jnp.zeros((), jnp.bfloat16)
    q_low = jnp.where(low, q_rot, zero)
    q_high = jnp.where(low, zero, q_rot)
    for i in range(slots // block):
        keys = block * (i + 1)
        k_part = k_rot[:keys]
        v_part = v[:keys]
        bias = bias_ref[i * block:(i + 1) * block, :keys]
        parts = []
        for qh in (q_low, q_high):
            scores = lax.dot_general(
                qh[i * block:(i + 1) * block], k_part, (((1,), (1,)), ((), ())),
                preferred_element_type=jnp.float32,
            )
            scores = scores + bias
            largest = jnp.max(scores, axis=-1, keepdims=True)
            raised = jnp.exp(scores - largest)
            total = jnp.sum(raised, axis=-1, keepdims=True)
            weights = (raised * (1.0 / total)).astype(jnp.bfloat16)
            parts.append(jnp.dot(weights, v_part, preferred_element_type=jnp.float32))
        context = jnp.where(low, parts[0], parts[1]).astype(jnp.bfloat16)
        acc_ref[i * block:(i + 1) * block, :] += jnp.dot(
            context, w_ref[...], preferred_element_type=jnp.float32
        )

    @pl.when(pl.program_id(0) == pl.num_programs(0) - 1)
    def _():
        out_ref[...] = acc_ref[...].astype(out_ref.dtype)


def attend(queries, projected_keys, projected_values, segment, out_weight, hidden_in):
    slot_capacity = queries.shape[0]
    slots = jnp.arange(slot_capacity, dtype=jnp.int32)
    begins = jnp.concatenate([jnp.ones((1,), dtype=jnp.bool_), segment[1:] != segment[:-1]])
    starts = lax.cummax(jnp.where(begins, slots, 0), axis=0)
    token_position = slots - starts
    cosine, sine = rotation_tables(token_position)
    turn = half_turn_matrix()
    def doubled(x):
        x = x.reshape(slot_capacity, KEY_VALUE_HEADS, 1, HEAD_SIZE)
        x = jnp.broadcast_to(x, (slot_capacity, KEY_VALUE_HEADS, 2, HEAD_SIZE))
        return x.reshape(slot_capacity, KEY_VALUE_HEADS * 2 * HEAD_SIZE)
    keys2 = doubled(projected_keys)
    values2 = doubled(projected_values)
    tiles = QUERY_HEADS * HEAD_SIZE // LANES
    per_kv = tiles // KEY_VALUE_HEADS
    full = lambda t: (0, 0)
    width = out_weight.shape[1]
    return pl.pallas_call(
        attention_kernel,
        grid=(tiles,),
        in_specs=[
            pl.BlockSpec((slot_capacity, LANES), lambda t: (0, t)),
            pl.BlockSpec((slot_capacity, LANES), lambda t: (0, t // per_kv)),
            pl.BlockSpec((slot_capacity, LANES), lambda t: (0, t // per_kv)),
            pl.BlockSpec((slot_capacity, LANES), full),
            pl.BlockSpec((slot_capacity, LANES), full),
            pl.BlockSpec((LANES, LANES), full),
            pl.BlockSpec((slot_capacity, 1), full),
            pl.BlockSpec((1, slot_capacity), full),
            pl.BlockSpec((1, slot_capacity), full),
            pl.BlockSpec((LANES, width), lambda t: (t, 0)),
            pl.BlockSpec((slot_capacity, width), full),
        ],
        out_specs=pl.BlockSpec((slot_capacity, width), full),
        out_shape=jax.ShapeDtypeStruct((slot_capacity, width), jnp.bfloat16),
        scratch_shapes=[
            pltpu.VMEM((slot_capacity, slot_capacity), jnp.float32),
            pltpu.VMEM((slot_capacity, width), jnp.float32),
        ],
        compiler_params=pltpu.CompilerParams(dimension_semantics=("arbitrary",)),
    )(
        queries, keys2, values2, cosine, sine, turn,
        segment.reshape(slot_capacity, 1), segment.reshape(1, slot_capacity),
        token_position.reshape(1, slot_capacity), out_weight, hidden_in,
    )


def normalize(rows, norm_gain):
    numbers = rows.astype(jnp.float32)
    factor = lax.rsqrt(jnp.mean(numbers * numbers, axis=-1, keepdims=True) + norm_eps)
    return (numbers * factor * norm_gain[None, :]).astype(jnp.bfloat16)


def project(attended_context, hidden_in, out_weight):
    return (
        hidden_in.astype(jnp.float32)
        + jnp.dot(attended_context, out_weight, preferred_element_type=jnp.float32)
    ).astype(jnp.bfloat16)


def ffn_rows(rows, gate_weight, up_weight, down_weight):
    gate = jnp.dot(rows, gate_weight, preferred_element_type=jnp.float32)
    upward = jnp.dot(rows, up_weight, preferred_element_type=jnp.float32)
    hidden = (jax.nn.silu(gate) * upward).astype(jnp.bfloat16)
    return jnp.dot(hidden, down_weight, preferred_element_type=jnp.float32).astype(jnp.bfloat16)


def feed_forward_direct(normed, gate_weight, up_weight, down_weight):
    groups = lax.axis_size("grp")
    rows = normed.shape[0]
    arrived = [
        lax.ppermute(normed, "grp", [(j, (j + k) % groups) for j in range(groups)])
        for k in range(1, groups)
    ]
    own = ffn_rows(normed, gate_weight, up_weight, down_weight)
    own, *arrived = lax.optimization_barrier((own, *arrived))
    others = ffn_rows(jnp.concatenate(arrived, axis=0), gate_weight, up_weight, down_weight)
    total = own.astype(jnp.float32)
    for k in range(1, groups):
        part = others[(k - 1) * rows:k * rows]
        part = lax.ppermute(part, "grp", [(j, (j - k) % groups) for j in range(groups)])
        total = total + part.astype(jnp.float32)
    return total


def feed_forward(normed, gate_weight, up_weight, down_weight):
    groups = lax.axis_size("grp")
    if groups != 4:
        return feed_forward_direct(normed, gate_weight, up_weight, down_weight)
    rows = normed.shape[0]
    half = rows // 2
    plus = [(j, (j + 1) % groups) for j in range(groups)]
    minus = [(j, (j - 1) % groups) for j in range(groups)]
    from_left = lax.ppermute(normed, "grp", plus)
    from_right = lax.ppermute(normed, "grp", minus)
    own = ffn_rows(normed, gate_weight, up_weight, down_weight)
    own, from_left, from_right = lax.optimization_barrier((own, from_left, from_right))
    far_first = lax.ppermute(from_left[:half], "grp", plus)
    far_second = lax.ppermute(from_right[half:], "grp", minus)
    near = ffn_rows(jnp.concatenate([from_left, from_right], axis=0), gate_weight, up_weight, down_weight)
    back_from_right = lax.ppermute(near[:rows], "grp", minus)
    back_from_left = lax.ppermute(near[rows:], "grp", plus)
    near, far_first, far_second = lax.optimization_barrier((near, far_first, far_second))
    far = ffn_rows(jnp.concatenate([far_first, far_second], axis=0), gate_weight, up_weight, down_weight)
    hop_first = lax.ppermute(lax.ppermute(far[:half], "grp", plus), "grp", plus)
    hop_second = lax.ppermute(lax.ppermute(far[half:], "grp", minus), "grp", minus)
    total = own.astype(jnp.float32) + back_from_right.astype(jnp.float32)
    total = total + back_from_left.astype(jnp.float32)
    return total + jnp.concatenate([hop_first, hop_second], axis=0).astype(jnp.float32)


def take_rows(table, index, valid):
    columns = jnp.arange(table.shape[0], dtype=jnp.int32)
    chosen = (index[:, None] == columns[None, :]) & valid[:, None]
    return jnp.dot(
        chosen.astype(table.dtype), table, preferred_element_type=jnp.float32
    ).astype(table.dtype)


def on_device(
    hidden_in,
    queries,
    projected_keys,
    projected_values,
    segment,
    live_rows,
    out_weight,
    norm_gain,
    gate_weight,
    up_weight,
    down_weight,
):
    slot_capacity = hidden_in.shape[0]
    rows = attend(
        queries, projected_keys, projected_values, segment.reshape(slot_capacity), out_weight, hidden_in
    )
    slots = jnp.arange(slot_capacity, dtype=jnp.int32)
    own_count = live_rows.reshape(())
    request_owners = lax.axis_size("req")
    own_index = lax.axis_index("req")
    block_rows = slot_capacity // request_owners
    counts = lax.all_to_all(
        jnp.broadcast_to(live_rows.reshape(1, 1), (request_owners, LANES)), "req", 0, 0, tiled=True
    )[:, 0]
    ends = jnp.cumsum(counts)
    firsts = ends - counts
    owner_ids = jnp.arange(request_owners, dtype=jnp.int32)
    own_first = jnp.sum(jnp.where(owner_ids == own_index, firsts, 0))
    own_shift = own_first % request_owners
    stream = jnp.arange(BAL, dtype=jnp.int32) * request_owners + own_index
    source = jnp.sum((ends[None, :] <= stream[:, None]).astype(jnp.int32), axis=1)
    source_first = jnp.sum(
        jnp.where(source[:, None] == owner_ids[None, :], firsts[None, :], 0), axis=1
    )
    pick = source * block_rows + (stream - source_first) // request_owners
    dest = jnp.arange(request_owners, dtype=jnp.int32)[:, None]
    blocks = jnp.arange(block_rows, dtype=jnp.int32)[None, :]
    send_row = blocks * request_owners + (dest - own_shift) % request_owners
    send_row = send_row.reshape(slot_capacity)
    outbound = take_rows(rows, send_row, send_row < own_count)
    arrived = lax.all_to_all(
        outbound.reshape(request_owners, block_rows, -1), "req", 0, 0, tiled=True
    )
    mixed = take_rows(arrived.reshape(slot_capacity, -1), pick, pick >= 0)
    normed = normalize(mixed, norm_gain)
    result = (
        mixed.astype(jnp.float32) + feed_forward(normed, gate_weight, up_weight, down_weight)
    ).astype(jnp.bfloat16)
    lanes = (own_index - firsts) % request_owners
    source_row = jnp.arange(block_rows, dtype=jnp.int32)[:, None] * request_owners + lanes[None, :]
    valid = source_row < counts[None, :]
    target = jnp.where(valid, (firsts[None, :] + source_row) // request_owners, 0)
    outgoing = take_rows(result, target.T.reshape(slot_capacity), valid.T.reshape(slot_capacity))
    returned = lax.all_to_all(
        outgoing.reshape(request_owners, block_rows, -1), "req", 0, 0, tiled=True
    ).reshape(slot_capacity, -1)
    back_row = ((slots % request_owners + own_shift) % request_owners) * block_rows + slots // request_owners
    return take_rows(returned, back_row, back_row >= 0)


def solution(mesh):
    placed = (
        P(("req", "grp"), None),
        P(("req", "grp"), None),
        P(("req", "grp"), None),
        P(("req", "grp"), None),
        P("req", "grp", None),
        P("req", "grp"),
        P(),
        P(),
        P(None, "grp"),
        P(None, "grp"),
        P("grp", None),
    )
    return jax.shard_map(
        on_device, mesh=mesh, in_specs=placed, out_specs=P(("req", "grp"), None), check_vma=False
    )
```

```python
import math

import jax
import jax.numpy as jnp
from jax import lax
from jax.experimental import pallas as pl
from jax.experimental.pallas import tpu as pltpu
from jax.sharding import PartitionSpec as P

QUERY_HEADS = 20
KEY_VALUE_HEADS = 5
HEAD_SIZE = 64
WINDOW = 128
SINK = 4
BAL = 128


rope_base = 10000.0
norm_eps = 1e-05
LANES = 128


def rotation_tables(token_position):
    half = HEAD_SIZE // 2
    inverse = rope_base ** (-(2.0 * jnp.arange(half, dtype=jnp.float32)) / HEAD_SIZE)
    angle = token_position.astype(jnp.float32)[:, None] * inverse[None, :]
    reps = LANES // half
    return jnp.tile(jnp.cos(angle), (1, reps)), jnp.tile(jnp.sin(angle), (1, reps))


def half_turn_matrix():
    lane = jnp.arange(LANES, dtype=jnp.int32)
    local = lane % HEAD_SIZE
    half = HEAD_SIZE // 2
    src = jnp.where(local < half, lane + half, lane - half)
    sign = jnp.where(local < half, -1.0, 1.0)
    turn = jnp.where(lane[:, None] == src[None, :], sign[None, :], 0.0)
    return turn.astype(jnp.bfloat16)


def attention_kernel(q_ref, k_ref, v_ref, cos_ref, sin_ref, turn_ref, segc_ref, segr_ref, posr_ref, w_ref, h_ref, out_ref, bias_ref, acc_ref):
    slots = q_ref.shape[0]
    block = LANES

    @pl.when(pl.program_id(0) == 0)
    def _():
        qi = lax.broadcasted_iota(jnp.int32, (slots, slots), 0)
        ki = lax.broadcasted_iota(jnp.int32, (slots, slots), 1)
        allowed = (segc_ref[...] == segr_ref[...]) & (ki <= qi)
        allowed = allowed & ((qi - ki < WINDOW) | (posr_ref[...] < SINK))
        bias_ref[...] = jnp.where(allowed, 0.0, -jnp.inf).astype(jnp.float32)
        acc_ref[...] = h_ref[...].astype(jnp.float32)

    cosine = cos_ref[...]
    sine = sin_ref[...]
    turn = turn_ref[...]

    def rotate(x):
        turned = jnp.dot(x, turn, preferred_element_type=jnp.float32)
        return (x.astype(jnp.float32) * cosine + turned * sine).astype(jnp.bfloat16)

    q_rot = rotate(q_ref[...]) * jnp.bfloat16(1.0 / math.sqrt(HEAD_SIZE))
    k_rot = rotate(k_ref[...])
    v = v_ref[...]
    lane = lax.broadcasted_iota(jnp.int32, (1, LANES), 1)
    low = lane < HEAD_SIZE
    zero = jnp.zeros((), jnp.bfloat16)
    q_low = jnp.where(low, q_rot, zero)
    q_high = jnp.where(low, zero, q_rot)
    for i in range(slots // block):
        keys = block * (i + 1)
        k_part = k_rot[:keys]
        v_part = v[:keys]
        bias = bias_ref[i * block:(i + 1) * block, :keys]
        parts = []
        for qh in (q_low, q_high):
            scores = lax.dot_general(
                qh[i * block:(i + 1) * block], k_part, (((1,), (1,)), ((), ())),
                preferred_element_type=jnp.float32,
            )
            scores = scores + bias
            largest = jnp.max(scores, axis=-1, keepdims=True)
            raised = jnp.exp(scores - largest)
            total = jnp.sum(raised, axis=-1, keepdims=True)
            weights = (raised * (1.0 / total)).astype(jnp.bfloat16)
            parts.append(jnp.dot(weights, v_part, preferred_element_type=jnp.float32))
        context = jnp.where(low, parts[0], parts[1]).astype(jnp.bfloat16)
        acc_ref[i * block:(i + 1) * block, :] += jnp.dot(
            context, w_ref[...], preferred_element_type=jnp.float32
        )

    @pl.when(pl.program_id(0) == pl.num_programs(0) - 1)
    def _():
        out_ref[...] = acc_ref[...].astype(out_ref.dtype)


def attend(queries, projected_keys, projected_values, segment, out_weight, hidden_in):
    slot_capacity = queries.shape[0]
    slots = jnp.arange(slot_capacity, dtype=jnp.int32)
    begins = jnp.concatenate([jnp.ones((1,), dtype=jnp.bool_), segment[1:] != segment[:-1]])
    starts = lax.cummax(jnp.where(begins, slots, 0), axis=0)
    token_position = slots - starts
    cosine, sine = rotation_tables(token_position)
    turn = half_turn_matrix()
    def doubled(x):
        x = x.reshape(slot_capacity, KEY_VALUE_HEADS, 1, HEAD_SIZE)
        x = jnp.broadcast_to(x, (slot_capacity, KEY_VALUE_HEADS, 2, HEAD_SIZE))
        return x.reshape(slot_capacity, KEY_VALUE_HEADS * 2 * HEAD_SIZE)
    keys2 = doubled(projected_keys)
    values2 = doubled(projected_values)
    tiles = QUERY_HEADS * HEAD_SIZE // LANES
    per_kv = tiles // KEY_VALUE_HEADS
    full = lambda t: (0, 0)
    width = out_weight.shape[1]
    return pl.pallas_call(
        attention_kernel,
        grid=(tiles,),
        in_specs=[
            pl.BlockSpec((slot_capacity, LANES), lambda t: (0, t)),
            pl.BlockSpec((slot_capacity, LANES), lambda t: (0, t // per_kv)),
            pl.BlockSpec((slot_capacity, LANES), lambda t: (0, t // per_kv)),
            pl.BlockSpec((slot_capacity, LANES), full),
            pl.BlockSpec((slot_capacity, LANES), full),
            pl.BlockSpec((LANES, LANES), full),
            pl.BlockSpec((slot_capacity, 1), full),
            pl.BlockSpec((1, slot_capacity), full),
            pl.BlockSpec((1, slot_capacity), full),
            pl.BlockSpec((LANES, width), lambda t: (t, 0)),
            pl.BlockSpec((slot_capacity, width), full),
        ],
        out_specs=pl.BlockSpec((slot_capacity, width), full),
        out_shape=jax.ShapeDtypeStruct((slot_capacity, width), jnp.bfloat16),
        scratch_shapes=[
            pltpu.VMEM((slot_capacity, slot_capacity), jnp.float32),
            pltpu.VMEM((slot_capacity, width), jnp.float32),
        ],
        compiler_params=pltpu.CompilerParams(dimension_semantics=("arbitrary",)),
    )(
        queries, keys2, values2, cosine, sine, turn,
        segment.reshape(slot_capacity, 1), segment.reshape(1, slot_capacity),
        token_position.reshape(1, slot_capacity), out_weight, hidden_in,
    )


def normalize(rows, norm_gain):
    numbers = rows.astype(jnp.float32)
    factor = lax.rsqrt(jnp.mean(numbers * numbers, axis=-1, keepdims=True) + norm_eps)
    return (numbers * factor * norm_gain[None, :]).astype(jnp.bfloat16)


def project(attended_context, hidden_in, out_weight):
    return (
        hidden_in.astype(jnp.float32)
        + jnp.dot(attended_context, out_weight, preferred_element_type=jnp.float32)
    ).astype(jnp.bfloat16)


def ffn_kernel(x_ref, g_ref, u_ref, d_ref, o_ref, acc_ref):
    step = pl.program_id(0)

    @pl.when(step == 0)
    def _():
        acc_ref[...] = jnp.zeros_like(acc_ref)

    x = x_ref[...]
    gate = jnp.dot(x, g_ref[...], preferred_element_type=jnp.float32)
    upward = jnp.dot(x, u_ref[...], preferred_element_type=jnp.float32)
    hidden = (gate / (1.0 + jnp.exp(-gate)) * upward).astype(jnp.bfloat16)
    acc_ref[...] += jnp.dot(hidden, d_ref[...], preferred_element_type=jnp.float32)

    @pl.when(step == pl.num_programs(0) - 1)
    def _():
        o_ref[...] = acc_ref[...].astype(o_ref.dtype)


def ffn_rows(rows, gate_weight, up_weight, down_weight):
    count, width = rows.shape
    units = gate_weight.shape[1]
    chunk = LANES
    flops = 6 * count * width * units
    moved = 2 * (3 * width * units + 2 * count * width)
    return pl.pallas_call(
        ffn_kernel,
        grid=(units // chunk,),
        in_specs=[
            pl.BlockSpec((count, width), lambda j: (0, 0)),
            pl.BlockSpec((width, chunk), lambda j: (0, j)),
            pl.BlockSpec((width, chunk), lambda j: (0, j)),
            pl.BlockSpec((chunk, width), lambda j: (j, 0)),
        ],
        out_specs=pl.BlockSpec((count, width), lambda j: (0, 0)),
        out_shape=jax.ShapeDtypeStruct((count, width), jnp.bfloat16),
        scratch_shapes=[pltpu.VMEM((count, width), jnp.float32)],
        compiler_params=pltpu.CompilerParams(dimension_semantics=("arbitrary",)),
        cost_estimate=pl.CostEstimate(flops=flops, transcendentals=count * units, bytes_accessed=moved),
    )(rows, gate_weight, up_weight, down_weight)


def feed_forward(normed, gate_weight, up_weight, down_weight):
    groups = lax.axis_size("grp")
    rows = normed.shape[0]
    arrived = [
        lax.ppermute(normed, "grp", [(j, (j + k) % groups) for j in range(groups)])
        for k in range(1, groups)
    ]
    own = ffn_rows(normed, gate_weight, up_weight, down_weight)
    own, *arrived = lax.optimization_barrier((own, *arrived))
    others = ffn_rows(jnp.concatenate(arrived, axis=0), gate_weight, up_weight, down_weight)
    total = own.astype(jnp.float32)
    for k in range(1, groups):
        part = others[(k - 1) * rows:k * rows]
        part = lax.ppermute(part, "grp", [(j, (j - k) % groups) for j in range(groups)])
        total = total + part.astype(jnp.float32)
    return total


def take_rows(table, index, valid):
    columns = jnp.arange(table.shape[0], dtype=jnp.int32)
    chosen = (index[:, None] == columns[None, :]) & valid[:, None]
    return jnp.dot(
        chosen.astype(table.dtype), table, preferred_element_type=jnp.float32
    ).astype(table.dtype)


def on_device(
    hidden_in,
    queries,
    projected_keys,
    projected_values,
    segment,
    live_rows,
    out_weight,
    norm_gain,
    gate_weight,
    up_weight,
    down_weight,
):
    slot_capacity = hidden_in.shape[0]
    rows = attend(
        queries, projected_keys, projected_values, segment.reshape(slot_capacity), out_weight, hidden_in
    )
    slots = jnp.arange(slot_capacity, dtype=jnp.int32)
    own_count = live_rows.reshape(())
    request_owners = lax.axis_size("req")
    own_index = lax.axis_index("req")
    block_rows = slot_capacity // request_owners
    counts = lax.all_to_all(
        jnp.broadcast_to(live_rows.reshape(1, 1), (request_owners, LANES)), "req", 0, 0, tiled=True
    )[:, 0]
    ends = jnp.cumsum(counts)
    firsts = ends - counts
    owner_ids = jnp.arange(request_owners, dtype=jnp.int32)
    own_first = jnp.sum(jnp.where(owner_ids == own_index, firsts, 0))
    own_shift = own_first % request_owners
    stream = jnp.arange(BAL, dtype=jnp.int32) * request_owners + own_index
    source = jnp.sum((ends[None, :] <= stream[:, None]).astype(jnp.int32), axis=1)
    source_first = jnp.sum(
        jnp.where(source[:, None] == owner_ids[None, :], firsts[None, :], 0), axis=1
    )
    pick = source * block_rows + (stream - source_first) // request_owners
    dest = jnp.arange(request_owners, dtype=jnp.int32)[:, None]
    blocks = jnp.arange(block_rows, dtype=jnp.int32)[None, :]
    send_row = blocks * request_owners + (dest - own_shift) % request_owners
    send_row = send_row.reshape(slot_capacity)
    outbound = take_rows(rows, send_row, send_row < own_count)
    arrived = lax.all_to_all(
        outbound.reshape(request_owners, block_rows, -1), "req", 0, 0, tiled=True
    )
    mixed = take_rows(arrived.reshape(slot_capacity, -1), pick, pick >= 0)
    normed = normalize(mixed, norm_gain)
    result = (
        mixed.astype(jnp.float32) + feed_forward(normed, gate_weight, up_weight, down_weight)
    ).astype(jnp.bfloat16)
    lanes = (own_index - firsts) % request_owners
    source_row = jnp.arange(block_rows, dtype=jnp.int32)[:, None] * request_owners + lanes[None, :]
    valid = source_row < counts[None, :]
    target = jnp.where(valid, (firsts[None, :] + source_row) // request_owners, 0)
    outgoing = take_rows(result, target.T.reshape(slot_capacity), valid.T.reshape(slot_capacity))
    returned = lax.all_to_all(
        outgoing.reshape(request_owners, block_rows, -1), "req", 0, 0, tiled=True
    ).reshape(slot_capacity, -1)
    back_row = ((slots % request_owners + own_shift) % request_owners) * block_rows + slots // request_owners
    return take_rows(returned, back_row, back_row >= 0)


def solution(mesh):
    placed = (
        P(("req", "grp"), None),
        P(("req", "grp"), None),
        P(("req", "grp"), None),
        P(("req", "grp"), None),
        P("req", "grp", None),
        P("req", "grp"),
        P(),
        P(),
        P(None, "grp"),
        P(None, "grp"),
        P("grp", None),
    )
    return jax.shard_map(
        on_device, mesh=mesh, in_specs=placed, out_specs=P(("req", "grp"), None), check_vma=False
    )
```

```python
import math

import jax
import jax.numpy as jnp
from jax import lax
from jax.experimental import pallas as pl
from jax.experimental.pallas import tpu as pltpu
from jax.sharding import PartitionSpec as P

QUERY_HEADS = 20
KEY_VALUE_HEADS = 5
HEAD_SIZE = 64
WINDOW = 128
SINK = 4
BAL = 128


rope_base = 10000.0
norm_eps = 1e-05
LANES = 128


def rotation_tables(token_position):
    half = HEAD_SIZE // 2
    inverse = rope_base ** (-(2.0 * jnp.arange(half, dtype=jnp.float32)) / HEAD_SIZE)
    angle = token_position.astype(jnp.float32)[:, None] * inverse[None, :]
    reps = LANES // half
    return jnp.tile(jnp.cos(angle), (1, reps)), jnp.tile(jnp.sin(angle), (1, reps))


def half_turn_matrix():
    lane = jnp.arange(LANES, dtype=jnp.int32)
    local = lane % HEAD_SIZE
    half = HEAD_SIZE // 2
    src = jnp.where(local < half, lane + half, lane - half)
    sign = jnp.where(local < half, -1.0, 1.0)
    turn = jnp.where(lane[:, None] == src[None, :], sign[None, :], 0.0)
    return turn.astype(jnp.bfloat16)


def attention_kernel(q_ref, k_ref, v_ref, cos_ref, sin_ref, turn_ref, segc_ref, segr_ref, posr_ref, w_ref, h_ref, out_ref, bias_ref, ctx_ref):
    slots = q_ref.shape[0]
    block = LANES

    @pl.when(pl.program_id(0) == 0)
    def _():
        qi = lax.broadcasted_iota(jnp.int32, (slots, slots), 0)
        ki = lax.broadcasted_iota(jnp.int32, (slots, slots), 1)
        allowed = (segc_ref[...] == segr_ref[...]) & (ki <= qi)
        allowed = allowed & ((qi - ki < WINDOW) | (posr_ref[...] < SINK))
        bias_ref[...] = jnp.where(allowed, 0.0, -jnp.inf).astype(jnp.float32)

    cosine = cos_ref[...]
    sine = sin_ref[...]
    turn = turn_ref[...]

    def rotate(x):
        turned = jnp.dot(x, turn, preferred_element_type=jnp.float32)
        return (x.astype(jnp.float32) * cosine + turned * sine).astype(jnp.bfloat16)

    q_rot = rotate(q_ref[...]) * jnp.bfloat16(1.0 / math.sqrt(HEAD_SIZE))
    k_rot = rotate(k_ref[...])
    v = v_ref[...]
    lane = lax.broadcasted_iota(jnp.int32, (1, LANES), 1)
    low = lane < HEAD_SIZE
    zero = jnp.zeros((), jnp.bfloat16)
    q_low = jnp.where(low, q_rot, zero)
    q_high = jnp.where(low, zero, q_rot)
    for i in range(slots // block):
        keys = block * (i + 1)
        k_part = k_rot[:keys]
        v_part = v[:keys]
        bias = bias_ref[i * block:(i + 1) * block, :keys]
        parts = []
        for qh in (q_low, q_high):
            scores = lax.dot_general(
                qh[i * block:(i + 1) * block], k_part, (((1,), (1,)), ((), ())),
                preferred_element_type=jnp.float32,
            )
            scores = scores + bias
            largest = jnp.max(scores, axis=-1, keepdims=True)
            raised = jnp.exp(scores - largest)
            total = jnp.sum(raised, axis=-1, keepdims=True)
            weights = (raised * (1.0 / total)).astype(jnp.bfloat16)
            parts.append(jnp.dot(weights, v_part, preferred_element_type=jnp.float32))
        context = jnp.where(low, parts[0], parts[1]).astype(jnp.bfloat16)
        ctx_ref[pl.program_id(0), i * block:(i + 1) * block, :] = context

    @pl.when(pl.program_id(0) == pl.num_programs(0) - 1)
    def _():
        heads = jnp.concatenate([ctx_ref[t] for t in range(ctx_ref.shape[0])], axis=1)
        mixed = h_ref[...].astype(jnp.float32) + jnp.dot(
            heads, w_ref[...], preferred_element_type=jnp.float32
        )
        out_ref[...] = mixed.astype(out_ref.dtype)


def attend(queries, projected_keys, projected_values, segment, out_weight, hidden_in):
    slot_capacity = queries.shape[0]
    slots = jnp.arange(slot_capacity, dtype=jnp.int32)
    begins = jnp.concatenate([jnp.ones((1,), dtype=jnp.bool_), segment[1:] != segment[:-1]])
    starts = lax.cummax(jnp.where(begins, slots, 0), axis=0)
    token_position = slots - starts
    cosine, sine = rotation_tables(token_position)
    turn = half_turn_matrix()
    def doubled(x):
        x = x.reshape(slot_capacity, KEY_VALUE_HEADS, 1, HEAD_SIZE)
        x = jnp.broadcast_to(x, (slot_capacity, KEY_VALUE_HEADS, 2, HEAD_SIZE))
        return x.reshape(slot_capacity, KEY_VALUE_HEADS * 2 * HEAD_SIZE)
    keys2 = doubled(projected_keys)
    values2 = doubled(projected_values)
    tiles = QUERY_HEADS * HEAD_SIZE // LANES
    per_kv = tiles // KEY_VALUE_HEADS
    full = lambda t: (0, 0)
    width = out_weight.shape[1]
    return pl.pallas_call(
        attention_kernel,
        grid=(tiles,),
        in_specs=[
            pl.BlockSpec((slot_capacity, LANES), lambda t: (0, t)),
            pl.BlockSpec((slot_capacity, LANES), lambda t: (0, t // per_kv)),
            pl.BlockSpec((slot_capacity, LANES), lambda t: (0, t // per_kv)),
            pl.BlockSpec((slot_capacity, LANES), full),
            pl.BlockSpec((slot_capacity, LANES), full),
            pl.BlockSpec((LANES, LANES), full),
            pl.BlockSpec((slot_capacity, 1), full),
            pl.BlockSpec((1, slot_capacity), full),
            pl.BlockSpec((1, slot_capacity), full),
            pl.BlockSpec((width, width), full),
            pl.BlockSpec((slot_capacity, width), full),
        ],
        out_specs=pl.BlockSpec((slot_capacity, width), full),
        out_shape=jax.ShapeDtypeStruct((slot_capacity, width), jnp.bfloat16),
        scratch_shapes=[
            pltpu.VMEM((slot_capacity, slot_capacity), jnp.float32),
            pltpu.VMEM((tiles, slot_capacity, LANES), jnp.bfloat16),
        ],
        compiler_params=pltpu.CompilerParams(dimension_semantics=("arbitrary",)),
    )(
        queries, keys2, values2, cosine, sine, turn,
        segment.reshape(slot_capacity, 1), segment.reshape(1, slot_capacity),
        token_position.reshape(1, slot_capacity), out_weight, hidden_in,
    )


def normalize(rows, norm_gain):
    numbers = rows.astype(jnp.float32)
    factor = lax.rsqrt(jnp.mean(numbers * numbers, axis=-1, keepdims=True) + norm_eps)
    return (numbers * factor * norm_gain[None, :]).astype(jnp.bfloat16)


def project(attended_context, hidden_in, out_weight):
    return (
        hidden_in.astype(jnp.float32)
        + jnp.dot(attended_context, out_weight, preferred_element_type=jnp.float32)
    ).astype(jnp.bfloat16)


def ffn_kernel(x_ref, g_ref, u_ref, d_ref, o_ref, acc_ref):
    step = pl.program_id(0)

    @pl.when(step == 0)
    def _():
        acc_ref[...] = jnp.zeros_like(acc_ref)

    x = x_ref[...]
    gate = jnp.dot(x, g_ref[...], preferred_element_type=jnp.float32)
    upward = jnp.dot(x, u_ref[...], preferred_element_type=jnp.float32)
    hidden = (gate / (1.0 + jnp.exp(-gate)) * upward).astype(jnp.bfloat16)
    acc_ref[...] += jnp.dot(hidden, d_ref[...], preferred_element_type=jnp.float32)

    @pl.when(step == pl.num_programs(0) - 1)
    def _():
        o_ref[...] = acc_ref[...].astype(o_ref.dtype)


def ffn_rows(rows, gate_weight, up_weight, down_weight):
    count, width = rows.shape
    units = gate_weight.shape[1]
    chunk = units
    flops = 6 * count * width * units
    moved = 2 * (3 * width * units + 2 * count * width)
    return pl.pallas_call(
        ffn_kernel,
        grid=(units // chunk,),
        in_specs=[
            pl.BlockSpec((count, width), lambda j: (0, 0)),
            pl.BlockSpec((width, chunk), lambda j: (0, j)),
            pl.BlockSpec((width, chunk), lambda j: (0, j)),
            pl.BlockSpec((chunk, width), lambda j: (j, 0)),
        ],
        out_specs=pl.BlockSpec((count, width), lambda j: (0, 0)),
        out_shape=jax.ShapeDtypeStruct((count, width), jnp.bfloat16),
        scratch_shapes=[pltpu.VMEM((count, width), jnp.float32)],
        compiler_params=pltpu.CompilerParams(dimension_semantics=("arbitrary",)),
        cost_estimate=pl.CostEstimate(flops=flops, transcendentals=count * units, bytes_accessed=moved),
    )(rows, gate_weight, up_weight, down_weight)


def feed_forward(normed, gate_weight, up_weight, down_weight):
    groups = lax.axis_size("grp")
    rows = normed.shape[0]
    arrived = [
        lax.ppermute(normed, "grp", [(j, (j + k) % groups) for j in range(groups)])
        for k in range(1, groups)
    ]
    own = ffn_rows(normed, gate_weight, up_weight, down_weight)
    own, *arrived = lax.optimization_barrier((own, *arrived))
    others = ffn_rows(jnp.concatenate(arrived, axis=0), gate_weight, up_weight, down_weight)
    total = own.astype(jnp.float32)
    for k in range(1, groups):
        part = others[(k - 1) * rows:k * rows]
        part = lax.ppermute(part, "grp", [(j, (j - k) % groups) for j in range(groups)])
        total = total + part.astype(jnp.float32)
    return total


def take_rows(table, index, valid):
    columns = jnp.arange(table.shape[0], dtype=jnp.int32)
    chosen = (index[:, None] == columns[None, :]) & valid[:, None]
    return jnp.dot(
        chosen.astype(table.dtype), table, preferred_element_type=jnp.float32
    ).astype(table.dtype)


def on_device(
    hidden_in,
    queries,
    projected_keys,
    projected_values,
    segment,
    live_rows,
    out_weight,
    norm_gain,
    gate_weight,
    up_weight,
    down_weight,
):
    slot_capacity = hidden_in.shape[0]
    rows = attend(
        queries, projected_keys, projected_values, segment.reshape(slot_capacity), out_weight, hidden_in
    )
    slots = jnp.arange(slot_capacity, dtype=jnp.int32)
    own_count = live_rows.reshape(())
    request_owners = lax.axis_size("req")
    own_index = lax.axis_index("req")
    block_rows = slot_capacity // request_owners
    counts = lax.all_to_all(
        jnp.broadcast_to(live_rows.reshape(1, 1), (request_owners, LANES)), "req", 0, 0, tiled=True
    )[:, 0]
    ends = jnp.cumsum(counts)
    firsts = ends - counts
    owner_ids = jnp.arange(request_owners, dtype=jnp.int32)
    own_first = jnp.sum(jnp.where(owner_ids == own_index, firsts, 0))
    own_shift = own_first % request_owners
    stream = jnp.arange(BAL, dtype=jnp.int32) * request_owners + own_index
    source = jnp.sum((ends[None, :] <= stream[:, None]).astype(jnp.int32), axis=1)
    source_first = jnp.sum(
        jnp.where(source[:, None] == owner_ids[None, :], firsts[None, :], 0), axis=1
    )
    pick = source * block_rows + (stream - source_first) // request_owners
    dest = jnp.arange(request_owners, dtype=jnp.int32)[:, None]
    blocks = jnp.arange(block_rows, dtype=jnp.int32)[None, :]
    send_row = blocks * request_owners + (dest - own_shift) % request_owners
    send_row = send_row.reshape(slot_capacity)
    outbound = take_rows(rows, send_row, send_row < own_count)
    arrived = lax.all_to_all(
        outbound.reshape(request_owners, block_rows, -1), "req", 0, 0, tiled=True
    )
    mixed = take_rows(arrived.reshape(slot_capacity, -1), pick, pick >= 0)
    normed = normalize(mixed, norm_gain)
    result = (
        mixed.astype(jnp.float32) + feed_forward(normed, gate_weight, up_weight, down_weight)
    ).astype(jnp.bfloat16)
    lanes = (own_index - firsts) % request_owners
    source_row = jnp.arange(block_rows, dtype=jnp.int32)[:, None] * request_owners + lanes[None, :]
    valid = source_row < counts[None, :]
    target = jnp.where(valid, (firsts[None, :] + source_row) // request_owners, 0)
    outgoing = take_rows(result, target.T.reshape(slot_capacity), valid.T.reshape(slot_capacity))
    returned = lax.all_to_all(
        outgoing.reshape(request_owners, block_rows, -1), "req", 0, 0, tiled=True
    ).reshape(slot_capacity, -1)
    back_row = ((slots % request_owners + own_shift) % request_owners) * block_rows + slots // request_owners
    return take_rows(returned, back_row, back_row >= 0)


def solution(mesh):
    placed = (
        P(("req", "grp"), None),
        P(("req", "grp"), None),
        P(("req", "grp"), None),
        P(("req", "grp"), None),
        P("req", "grp", None),
        P("req", "grp"),
        P(),
        P(),
        P(None, "grp"),
        P(None, "grp"),
        P("grp", None),
    )
    return jax.shard_map(
        on_device, mesh=mesh, in_specs=placed, out_specs=P(("req", "grp"), None), check_vma=False
    )
```

```python
import math

import jax
import jax.numpy as jnp
from jax import lax
from jax.experimental import pallas as pl
from jax.experimental.pallas import tpu as pltpu
from jax.sharding import PartitionSpec as P

QUERY_HEADS = 20
KEY_VALUE_HEADS = 5
HEAD_SIZE = 64
WINDOW = 128
SINK = 4
BAL = 128


rope_base = 10000.0
norm_eps = 1e-05
LANES = 128


def rotation_tables(token_position):
    half = HEAD_SIZE // 2
    inverse = rope_base ** (-(2.0 * jnp.arange(half, dtype=jnp.float32)) / HEAD_SIZE)
    angle = token_position.astype(jnp.float32)[:, None] * inverse[None, :]
    reps = LANES // half
    return jnp.tile(jnp.cos(angle), (1, reps)), jnp.tile(jnp.sin(angle), (1, reps))


def half_turn_matrix():
    lane = jnp.arange(LANES, dtype=jnp.int32)
    local = lane % HEAD_SIZE
    half = HEAD_SIZE // 2
    src = jnp.where(local < half, lane + half, lane - half)
    sign = jnp.where(local < half, -1.0, 1.0)
    turn = jnp.where(lane[:, None] == src[None, :], sign[None, :], 0.0)
    return turn.astype(jnp.bfloat16)


def attention_kernel(q_ref, k_ref, v_ref, pick_ref, cos_ref, sin_ref, turn_ref, segc_ref, segr_ref, posr_ref, w_ref, h_ref, out_ref, bias_ref, ctx_ref):
    slots = q_ref.shape[0]
    block = LANES

    @pl.when(pl.program_id(0) == 0)
    def _():
        qi = lax.broadcasted_iota(jnp.int32, (slots, slots), 0)
        ki = lax.broadcasted_iota(jnp.int32, (slots, slots), 1)
        allowed = (segc_ref[...] == segr_ref[...]) & (ki <= qi)
        allowed = allowed & ((qi - ki < WINDOW) | (posr_ref[...] < SINK))
        bias_ref[...] = jnp.where(allowed, 0.0, -jnp.inf).astype(jnp.float32)

    cosine = cos_ref[...]
    sine = sin_ref[...]
    turn = turn_ref[...]

    def rotate(x):
        turned = jnp.dot(x, turn, preferred_element_type=jnp.float32)
        return (x.astype(jnp.float32) * cosine + turned * sine).astype(jnp.bfloat16)

    q_rot = rotate(q_ref[...]) * jnp.bfloat16(1.0 / math.sqrt(HEAD_SIZE))
    pick = pick_ref[...]
    k_rot = rotate(jnp.dot(k_ref[...], pick, preferred_element_type=jnp.float32).astype(jnp.bfloat16))
    v = jnp.dot(v_ref[...], pick, preferred_element_type=jnp.float32).astype(jnp.bfloat16)
    lane = lax.broadcasted_iota(jnp.int32, (1, LANES), 1)
    low = lane < HEAD_SIZE
    zero = jnp.zeros((), jnp.bfloat16)
    q_low = jnp.where(low, q_rot, zero)
    q_high = jnp.where(low, zero, q_rot)
    for i in range(slots // block):
        keys = block * (i + 1)
        k_part = k_rot[:keys]
        v_part = v[:keys]
        bias = bias_ref[i * block:(i + 1) * block, :keys]
        parts = []
        for qh in (q_low, q_high):
            scores = lax.dot_general(
                qh[i * block:(i + 1) * block], k_part, (((1,), (1,)), ((), ())),
                preferred_element_type=jnp.float32,
            )
            scores = scores + bias
            largest = jnp.max(scores, axis=-1, keepdims=True)
            raised = jnp.exp(scores - largest)
            total = jnp.sum(raised, axis=-1, keepdims=True)
            weights = (raised * (1.0 / total)).astype(jnp.bfloat16)
            parts.append(jnp.dot(weights, v_part, preferred_element_type=jnp.float32))
        context = jnp.where(low, parts[0], parts[1]).astype(jnp.bfloat16)
        ctx_ref[pl.program_id(0), i * block:(i + 1) * block, :] = context

    @pl.when(pl.program_id(0) == pl.num_programs(0) - 1)
    def _():
        heads = jnp.concatenate([ctx_ref[t] for t in range(ctx_ref.shape[0])], axis=1)
        mixed = h_ref[...].astype(jnp.float32) + jnp.dot(
            heads, w_ref[...], preferred_element_type=jnp.float32
        )
        out_ref[...] = mixed.astype(out_ref.dtype)


def attend(queries, projected_keys, projected_values, segment, out_weight, hidden_in):
    slot_capacity = queries.shape[0]
    slots = jnp.arange(slot_capacity, dtype=jnp.int32)
    begins = jnp.concatenate([jnp.ones((1,), dtype=jnp.bool_), segment[1:] != segment[:-1]])
    starts = lax.cummax(jnp.where(begins, slots, 0), axis=0)
    token_position = slots - starts
    cosine, sine = rotation_tables(token_position)
    turn = half_turn_matrix()
    padded = -projected_keys.shape[1] % LANES
    keys2 = jnp.pad(projected_keys, ((0, 0), (0, padded)))
    values2 = jnp.pad(projected_values, ((0, 0), (0, padded)))
    lane = jnp.arange(LANES, dtype=jnp.int32)
    halves = jnp.arange(LANES // HEAD_SIZE, dtype=jnp.int32)[:, None, None]
    picks = (lane[None, :, None] == halves * HEAD_SIZE + lane[None, None, :] % HEAD_SIZE)
    picks = picks.astype(jnp.bfloat16)
    tiles = QUERY_HEADS * HEAD_SIZE // LANES
    per_kv = tiles // KEY_VALUE_HEADS
    full = lambda t: (0, 0)
    width = out_weight.shape[1]
    return pl.pallas_call(
        attention_kernel,
        grid=(tiles,),
        in_specs=[
            pl.BlockSpec((slot_capacity, LANES), lambda t: (0, t)),
            pl.BlockSpec((slot_capacity, LANES), lambda t: (0, t // per_kv // 2)),
            pl.BlockSpec((slot_capacity, LANES), lambda t: (0, t // per_kv // 2)),
            pl.BlockSpec((None, LANES, LANES), lambda t: (t // per_kv % 2, 0, 0)),
            pl.BlockSpec((slot_capacity, LANES), full),
            pl.BlockSpec((slot_capacity, LANES), full),
            pl.BlockSpec((LANES, LANES), full),
            pl.BlockSpec((slot_capacity, 1), full),
            pl.BlockSpec((1, slot_capacity), full),
            pl.BlockSpec((1, slot_capacity), full),
            pl.BlockSpec((width, width), full),
            pl.BlockSpec((slot_capacity, width), full),
        ],
        out_specs=pl.BlockSpec((slot_capacity, width), full),
        out_shape=jax.ShapeDtypeStruct((slot_capacity, width), jnp.bfloat16),
        scratch_shapes=[
            pltpu.VMEM((slot_capacity, slot_capacity), jnp.float32),
            pltpu.VMEM((tiles, slot_capacity, LANES), jnp.bfloat16),
        ],
        compiler_params=pltpu.CompilerParams(dimension_semantics=("arbitrary",)),
    )(
        queries, keys2, values2, picks, cosine, sine, turn,
        segment.reshape(slot_capacity, 1), segment.reshape(1, slot_capacity),
        token_position.reshape(1, slot_capacity), out_weight, hidden_in,
    )


def normalize(rows, norm_gain):
    numbers = rows.astype(jnp.float32)
    factor = lax.rsqrt(jnp.mean(numbers * numbers, axis=-1, keepdims=True) + norm_eps)
    return (numbers * factor * norm_gain[None, :]).astype(jnp.bfloat16)


def project(attended_context, hidden_in, out_weight):
    return (
        hidden_in.astype(jnp.float32)
        + jnp.dot(attended_context, out_weight, preferred_element_type=jnp.float32)
    ).astype(jnp.bfloat16)


def ffn_kernel(x_ref, g_ref, u_ref, d_ref, o_ref, acc_ref):
    step = pl.program_id(0)

    @pl.when(step == 0)
    def _():
        acc_ref[...] = jnp.zeros_like(acc_ref)

    x = x_ref[...]
    gate = jnp.dot(x, g_ref[...], preferred_element_type=jnp.float32)
    upward = jnp.dot(x, u_ref[...], preferred_element_type=jnp.float32)
    hidden = (gate / (1.0 + jnp.exp(-gate)) * upward).astype(jnp.bfloat16)
    acc_ref[...] += jnp.dot(hidden, d_ref[...], preferred_element_type=jnp.float32)

    @pl.when(step == pl.num_programs(0) - 1)
    def _():
        o_ref[...] = acc_ref[...].astype(o_ref.dtype)


def ffn_rows(rows, gate_weight, up_weight, down_weight):
    count, width = rows.shape
    units = gate_weight.shape[1]
    chunk = units
    flops = 6 * count * width * units
    moved = 2 * (3 * width * units + 2 * count * width)
    return pl.pallas_call(
        ffn_kernel,
        grid=(units // chunk,),
        in_specs=[
            pl.BlockSpec((count, width), lambda j: (0, 0)),
            pl.BlockSpec((width, chunk), lambda j: (0, j)),
            pl.BlockSpec((width, chunk), lambda j: (0, j)),
            pl.BlockSpec((chunk, width), lambda j: (j, 0)),
        ],
        out_specs=pl.BlockSpec((count, width), lambda j: (0, 0)),
        out_shape=jax.ShapeDtypeStruct((count, width), jnp.bfloat16),
        scratch_shapes=[pltpu.VMEM((count, width), jnp.float32)],
        compiler_params=pltpu.CompilerParams(dimension_semantics=("arbitrary",)),
        cost_estimate=pl.CostEstimate(flops=flops, transcendentals=count * units, bytes_accessed=moved),
    )(rows, gate_weight, up_weight, down_weight)


def feed_forward(normed, gate_weight, up_weight, down_weight):
    groups = lax.axis_size("grp")
    rows = normed.shape[0]
    arrived = [
        lax.ppermute(normed, "grp", [(j, (j + k) % groups) for j in range(groups)])
        for k in range(1, groups)
    ]
    own = ffn_rows(normed, gate_weight, up_weight, down_weight)
    own, *arrived = lax.optimization_barrier((own, *arrived))
    others = ffn_rows(jnp.concatenate(arrived, axis=0), gate_weight, up_weight, down_weight)
    total = own.astype(jnp.float32)
    for k in range(1, groups):
        part = others[(k - 1) * rows:k * rows]
        part = lax.ppermute(part, "grp", [(j, (j - k) % groups) for j in range(groups)])
        total = total + part.astype(jnp.float32)
    return total


def take_rows(table, index, valid):
    columns = jnp.arange(table.shape[0], dtype=jnp.int32)
    chosen = (index[:, None] == columns[None, :]) & valid[:, None]
    return jnp.dot(
        chosen.astype(table.dtype), table, preferred_element_type=jnp.float32
    ).astype(table.dtype)


def on_device(
    hidden_in,
    queries,
    projected_keys,
    projected_values,
    segment,
    live_rows,
    out_weight,
    norm_gain,
    gate_weight,
    up_weight,
    down_weight,
):
    slot_capacity = hidden_in.shape[0]
    rows = attend(
        queries, projected_keys, projected_values, segment.reshape(slot_capacity), out_weight, hidden_in
    )
    slots = jnp.arange(slot_capacity, dtype=jnp.int32)
    own_count = live_rows.reshape(())
    request_owners = lax.axis_size("req")
    own_index = lax.axis_index("req")
    block_rows = slot_capacity // request_owners
    counts = lax.all_to_all(
        jnp.broadcast_to(live_rows.reshape(1, 1), (request_owners, LANES)), "req", 0, 0, tiled=True
    )[:, 0]
    ends = jnp.cumsum(counts)
    firsts = ends - counts
    owner_ids = jnp.arange(request_owners, dtype=jnp.int32)
    own_first = jnp.sum(jnp.where(owner_ids == own_index, firsts, 0))
    own_shift = own_first % request_owners
    stream = jnp.arange(BAL, dtype=jnp.int32) * request_owners + own_index
    source = jnp.sum((ends[None, :] <= stream[:, None]).astype(jnp.int32), axis=1)
    source_first = jnp.sum(
        jnp.where(source[:, None] == owner_ids[None, :], firsts[None, :], 0), axis=1
    )
    pick = source * block_rows + (stream - source_first) // request_owners
    dest = jnp.arange(request_owners, dtype=jnp.int32)[:, None]
    blocks = jnp.arange(block_rows, dtype=jnp.int32)[None, :]
    send_row = blocks * request_owners + (dest - own_shift) % request_owners
    send_row = send_row.reshape(slot_capacity)
    outbound = take_rows(rows, send_row, send_row < own_count)
    arrived = lax.all_to_all(
        outbound.reshape(request_owners, block_rows, -1), "req", 0, 0, tiled=True
    )
    mixed = take_rows(arrived.reshape(slot_capacity, -1), pick, pick >= 0)
    normed = normalize(mixed, norm_gain)
    result = (
        mixed.astype(jnp.float32) + feed_forward(normed, gate_weight, up_weight, down_weight)
    ).astype(jnp.bfloat16)
    lanes = (own_index - firsts) % request_owners
    source_row = jnp.arange(block_rows, dtype=jnp.int32)[:, None] * request_owners + lanes[None, :]
    valid = source_row < counts[None, :]
    target = jnp.where(valid, (firsts[None, :] + source_row) // request_owners, 0)
    outgoing = take_rows(result, target.T.reshape(slot_capacity), valid.T.reshape(slot_capacity))
    returned = lax.all_to_all(
        outgoing.reshape(request_owners, block_rows, -1), "req", 0, 0, tiled=True
    ).reshape(slot_capacity, -1)
    back_row = ((slots % request_owners + own_shift) % request_owners) * block_rows + slots // request_owners
    return take_rows(returned, back_row, back_row >= 0)


def solution(mesh):
    placed = (
        P(("req", "grp"), None),
        P(("req", "grp"), None),
        P(("req", "grp"), None),
        P(("req", "grp"), None),
        P("req", "grp", None),
        P("req", "grp"),
        P(),
        P(),
        P(None, "grp"),
        P(None, "grp"),
        P("grp", None),
    )
    return jax.shard_map(
        on_device, mesh=mesh, in_specs=placed, out_specs=P(("req", "grp"), None), check_vma=False
    )
```

```python
import math

import jax
import jax.numpy as jnp
from jax import lax
from jax.experimental import pallas as pl
from jax.experimental.pallas import tpu as pltpu
from jax.sharding import PartitionSpec as P

QUERY_HEADS = 20
KEY_VALUE_HEADS = 5
HEAD_SIZE = 64
WINDOW = 128
SINK = 4
BAL = 128


rope_base = 10000.0
norm_eps = 1e-05
LANES = 128


def rotation_tables(token_position):
    half = HEAD_SIZE // 2
    inverse = rope_base ** (-(2.0 * jnp.arange(half, dtype=jnp.float32)) / HEAD_SIZE)
    angle = token_position.astype(jnp.float32)[:, None] * inverse[None, :]
    reps = LANES // half
    return jnp.tile(jnp.cos(angle), (1, reps)), jnp.tile(jnp.sin(angle), (1, reps))


def half_turn_matrix():
    lane = jnp.arange(LANES, dtype=jnp.int32)
    local = lane % HEAD_SIZE
    half = HEAD_SIZE // 2
    src = jnp.where(local < half, lane + half, lane - half)
    sign = jnp.where(local < half, -1.0, 1.0)
    turn = jnp.where(lane[:, None] == src[None, :], sign[None, :], 0.0)
    return turn.astype(jnp.bfloat16)


def attention_kernel(q_ref, k_ref, v_ref, cos_ref, sin_ref, segc_ref, segr_ref, posr_ref, w_ref, h_ref, out_ref, bias_ref, ctx_ref):
    slots = q_ref.shape[0]
    block = LANES

    @pl.when(pl.program_id(0) == 0)
    def _():
        qi = lax.broadcasted_iota(jnp.int32, (slots, slots), 0)
        ki = lax.broadcasted_iota(jnp.int32, (slots, slots), 1)
        allowed = (segc_ref[...] == segr_ref[...]) & (ki <= qi)
        allowed = allowed & ((qi - ki < WINDOW) | (posr_ref[...] < SINK))
        bias_ref[...] = jnp.where(allowed, 0.0, -jnp.inf).astype(jnp.float32)

    cosine = cos_ref[...]
    sine = sin_ref[...]
    src = lax.broadcasted_iota(jnp.int32, (LANES, LANES), 0)
    dst = lax.broadcasted_iota(jnp.int32, (LANES, LANES), 1)
    first = dst % HEAD_SIZE < HEAD_SIZE // 2
    turn = jnp.where(
        first & (src == dst + HEAD_SIZE // 2), -1.0, jnp.where(~first & (src == dst - HEAD_SIZE // 2), 1.0, 0.0)
    ).astype(jnp.bfloat16)

    def rotate(x):
        turned = jnp.dot(x, turn, preferred_element_type=jnp.float32)
        return (x.astype(jnp.float32) * cosine + turned * sine).astype(jnp.bfloat16)

    q_rot = rotate(q_ref[...]) * jnp.bfloat16(1.0 / math.sqrt(HEAD_SIZE))
    k_rot = rotate(k_ref[...])
    v = v_ref[...]
    lane = lax.broadcasted_iota(jnp.int32, (1, LANES), 1)
    low = lane < HEAD_SIZE
    zero = jnp.zeros((), jnp.bfloat16)
    q_low = jnp.where(low, q_rot, zero)
    q_high = jnp.where(low, zero, q_rot)
    for i in range(slots // block):
        keys = block * (i + 1)
        k_part = k_rot[:keys]
        v_part = v[:keys]
        bias = bias_ref[i * block:(i + 1) * block, :keys]
        parts = []
        for qh in (q_low, q_high):
            scores = lax.dot_general(
                qh[i * block:(i + 1) * block], k_part, (((1,), (1,)), ((), ())),
                preferred_element_type=jnp.float32,
            )
            scores = scores + bias
            largest = jnp.max(scores, axis=-1, keepdims=True)
            raised = jnp.exp(scores - largest)
            total = jnp.sum(raised, axis=-1, keepdims=True)
            weights = (raised * (1.0 / total)).astype(jnp.bfloat16)
            parts.append(jnp.dot(weights, v_part, preferred_element_type=jnp.float32))
        context = jnp.where(low, parts[0], parts[1]).astype(jnp.bfloat16)
        ctx_ref[pl.program_id(0), i * block:(i + 1) * block, :] = context

    @pl.when(pl.program_id(0) == pl.num_programs(0) - 1)
    def _():
        heads = jnp.concatenate([ctx_ref[t] for t in range(ctx_ref.shape[0])], axis=1)
        mixed = h_ref[...].astype(jnp.float32) + jnp.dot(
            heads, w_ref[...], preferred_element_type=jnp.float32
        )
        out_ref[...] = mixed.astype(out_ref.dtype)


def attend(queries, projected_keys, projected_values, segment, out_weight, hidden_in):
    slot_capacity = queries.shape[0]
    slots = jnp.arange(slot_capacity, dtype=jnp.int32)
    begins = jnp.concatenate([jnp.ones((1,), dtype=jnp.bool_), segment[1:] != segment[:-1]])
    starts = lax.cummax(jnp.where(begins, slots, 0), axis=0)
    token_position = slots - starts
    cosine, sine = rotation_tables(token_position)
    def doubled(x):
        x = x.reshape(slot_capacity, KEY_VALUE_HEADS, 1, HEAD_SIZE)
        x = jnp.broadcast_to(x, (slot_capacity, KEY_VALUE_HEADS, 2, HEAD_SIZE))
        return x.reshape(slot_capacity, KEY_VALUE_HEADS * 2 * HEAD_SIZE)
    keys2 = doubled(projected_keys)
    values2 = doubled(projected_values)
    tiles = QUERY_HEADS * HEAD_SIZE // LANES
    per_kv = tiles // KEY_VALUE_HEADS
    full = lambda t: (0, 0)
    width = out_weight.shape[1]
    return pl.pallas_call(
        attention_kernel,
        grid=(tiles,),
        in_specs=[
            pl.BlockSpec((slot_capacity, LANES), lambda t: (0, t)),
            pl.BlockSpec((slot_capacity, LANES), lambda t: (0, t // per_kv)),
            pl.BlockSpec((slot_capacity, LANES), lambda t: (0, t // per_kv)),
            pl.BlockSpec((slot_capacity, LANES), full),
            pl.BlockSpec((slot_capacity, LANES), full),
            pl.BlockSpec((slot_capacity, 1), full),
            pl.BlockSpec((1, slot_capacity), full),
            pl.BlockSpec((1, slot_capacity), full),
            pl.BlockSpec((width, width), full),
            pl.BlockSpec((slot_capacity, width), full),
        ],
        out_specs=pl.BlockSpec((slot_capacity, width), full),
        out_shape=jax.ShapeDtypeStruct((slot_capacity, width), jnp.bfloat16),
        scratch_shapes=[
            pltpu.VMEM((slot_capacity, slot_capacity), jnp.float32),
            pltpu.VMEM((tiles, slot_capacity, LANES), jnp.bfloat16),
        ],
        compiler_params=pltpu.CompilerParams(dimension_semantics=("arbitrary",)),
    )(
        queries, keys2, values2, cosine, sine,
        segment.reshape(slot_capacity, 1), segment.reshape(1, slot_capacity),
        token_position.reshape(1, slot_capacity), out_weight, hidden_in,
    )


def normalize(rows, norm_gain):
    numbers = rows.astype(jnp.float32)
    factor = lax.rsqrt(jnp.mean(numbers * numbers, axis=-1, keepdims=True) + norm_eps)
    return (numbers * factor * norm_gain[None, :]).astype(jnp.bfloat16)


def project(attended_context, hidden_in, out_weight):
    return (
        hidden_in.astype(jnp.float32)
        + jnp.dot(attended_context, out_weight, preferred_element_type=jnp.float32)
    ).astype(jnp.bfloat16)


def ffn_kernel(*refs):
    *x_refs, g_ref, u_ref, d_ref, o_ref = refs
    x = jnp.concatenate([r[...] for r in x_refs], axis=0) if len(x_refs) > 1 else x_refs[0][...]
    gate = jnp.dot(x, g_ref[...], preferred_element_type=jnp.float32)
    upward = jnp.dot(x, u_ref[...], preferred_element_type=jnp.float32)
    hidden = (gate / (1.0 + jnp.exp(-gate)) * upward).astype(jnp.bfloat16)
    o_ref[...] = jnp.dot(hidden, d_ref[...], preferred_element_type=jnp.float32).astype(o_ref.dtype)


def ffn_rows(blocks, gate_weight, up_weight, down_weight):
    width = blocks[0].shape[1]
    count = sum(b.shape[0] for b in blocks)
    units = gate_weight.shape[1]
    flops = 6 * count * width * units
    moved = 2 * (3 * width * units + 2 * count * width)
    return pl.pallas_call(
        ffn_kernel,
        grid=(1,),
        in_specs=[pl.BlockSpec(b.shape, lambda j: (0, 0)) for b in blocks] + [
            pl.BlockSpec((width, units), lambda j: (0, 0)),
            pl.BlockSpec((width, units), lambda j: (0, 0)),
            pl.BlockSpec((units, width), lambda j: (0, 0)),
        ],
        out_specs=pl.BlockSpec((count, width), lambda j: (0, 0)),
        out_shape=jax.ShapeDtypeStruct((count, width), jnp.bfloat16),
        compiler_params=pltpu.CompilerParams(dimension_semantics=("arbitrary",)),
        cost_estimate=pl.CostEstimate(flops=flops, transcendentals=count * units, bytes_accessed=moved),
    )(*blocks, gate_weight, up_weight, down_weight)


def feed_forward(normed, gate_weight, up_weight, down_weight):
    groups = lax.axis_size("grp")
    rows = normed.shape[0]
    arrived = [
        lax.ppermute(normed, "grp", [(j, (j + k) % groups) for j in range(groups)])
        for k in range(1, groups)
    ]
    own = ffn_rows([normed], gate_weight, up_weight, down_weight)
    own, *arrived = lax.optimization_barrier((own, *arrived))
    others = ffn_rows(arrived, gate_weight, up_weight, down_weight)
    total = own.astype(jnp.float32)
    for k in range(1, groups):
        part = others[(k - 1) * rows:k * rows]
        part = lax.ppermute(part, "grp", [(j, (j - k) % groups) for j in range(groups)])
        total = total + part.astype(jnp.float32)
    return total


def take_rows(table, index, valid):
    columns = jnp.arange(table.shape[0], dtype=jnp.int32)
    chosen = (index[:, None] == columns[None, :]) & valid[:, None]
    return jnp.dot(
        chosen.astype(table.dtype), table, preferred_element_type=jnp.float32
    ).astype(table.dtype)


def on_device(
    hidden_in,
    queries,
    projected_keys,
    projected_values,
    segment,
    live_rows,
    out_weight,
    norm_gain,
    gate_weight,
    up_weight,
    down_weight,
):
    slot_capacity = hidden_in.shape[0]
    rows = attend(
        queries, projected_keys, projected_values, segment.reshape(slot_capacity), out_weight, hidden_in
    )
    slots = jnp.arange(slot_capacity, dtype=jnp.int32)
    own_count = live_rows.reshape(())
    request_owners = lax.axis_size("req")
    own_index = lax.axis_index("req")
    block_rows = slot_capacity // request_owners
    counts = lax.all_to_all(
        jnp.broadcast_to(live_rows.reshape(1, 1), (request_owners, LANES)), "req", 0, 0, tiled=True
    )[:, 0]
    ends = jnp.cumsum(counts)
    firsts = ends - counts
    owner_ids = jnp.arange(request_owners, dtype=jnp.int32)
    own_first = jnp.sum(jnp.where(owner_ids == own_index, firsts, 0))
    own_shift = own_first % request_owners
    stream = jnp.arange(BAL, dtype=jnp.int32) * request_owners + own_index
    source = jnp.sum((ends[None, :] <= stream[:, None]).astype(jnp.int32), axis=1)
    source_first = jnp.sum(
        jnp.where(source[:, None] == owner_ids[None, :], firsts[None, :], 0), axis=1
    )
    pick = source * block_rows + (stream - source_first) // request_owners
    dest = jnp.arange(request_owners, dtype=jnp.int32)[:, None]
    blocks = jnp.arange(block_rows, dtype=jnp.int32)[None, :]
    send_row = blocks * request_owners + (dest - own_shift) % request_owners
    send_row = send_row.reshape(slot_capacity)
    outbound = take_rows(rows, send_row, send_row < own_count)
    arrived = lax.all_to_all(
        outbound.reshape(request_owners, block_rows, -1), "req", 0, 0, tiled=True
    )
    mixed = take_rows(arrived.reshape(slot_capacity, -1), pick, pick >= 0)
    normed = normalize(mixed, norm_gain)
    result = (
        mixed.astype(jnp.float32) + feed_forward(normed, gate_weight, up_weight, down_weight)
    ).astype(jnp.bfloat16)
    lanes = (own_index - firsts) % request_owners
    source_row = jnp.arange(block_rows, dtype=jnp.int32)[:, None] * request_owners + lanes[None, :]
    valid = source_row < counts[None, :]
    target = jnp.where(valid, (firsts[None, :] + source_row) // request_owners, 0)
    outgoing = take_rows(result, target.T.reshape(slot_capacity), valid.T.reshape(slot_capacity))
    returned = lax.all_to_all(
        outgoing.reshape(request_owners, block_rows, -1), "req", 0, 0, tiled=True
    ).reshape(slot_capacity, -1)
    back_row = ((slots % request_owners + own_shift) % request_owners) * block_rows + slots // request_owners
    return take_rows(returned, back_row, back_row >= 0)


def solution(mesh):
    placed = (
        P(("req", "grp"), None),
        P(("req", "grp"), None),
        P(("req", "grp"), None),
        P(("req", "grp"), None),
        P("req", "grp", None),
        P("req", "grp"),
        P(),
        P(),
        P(None, "grp"),
        P(None, "grp"),
        P("grp", None),
    )
    return jax.shard_map(
        on_device, mesh=mesh, in_specs=placed, out_specs=P(("req", "grp"), None), check_vma=False
    )
```

```python
import math

import jax
import jax.numpy as jnp
from jax import lax
from jax.experimental import pallas as pl
from jax.experimental.pallas import tpu as pltpu
from jax.sharding import PartitionSpec as P

QUERY_HEADS = 20
KEY_VALUE_HEADS = 5
HEAD_SIZE = 64
WINDOW = 128
SINK = 4
BAL = 128


rope_base = 10000.0
norm_eps = 1e-05
LANES = 128


def rotation_tables(token_position):
    half = HEAD_SIZE // 2
    inverse = rope_base ** (-(2.0 * jnp.arange(half, dtype=jnp.float32)) / HEAD_SIZE)
    inverse = jnp.tile(inverse, LANES // half)
    angle = token_position.astype(jnp.float32)[:, None] * inverse[None, :]
    return jnp.cos(angle), jnp.sin(angle)


def half_turn_matrix():
    lane = jnp.arange(LANES, dtype=jnp.int32)
    local = lane % HEAD_SIZE
    half = HEAD_SIZE // 2
    src = jnp.where(local < half, lane + half, lane - half)
    sign = jnp.where(local < half, -1.0, 1.0)
    turn = jnp.where(lane[:, None] == src[None, :], sign[None, :], 0.0)
    return turn.astype(jnp.bfloat16)


def attention_kernel(q_ref, k_ref, v_ref, cos_ref, sin_ref, segc_ref, segr_ref, posr_ref, w_ref, h_ref, out_ref, bias_ref, ctx_ref):
    slots = q_ref.shape[0]
    block = LANES

    @pl.when(pl.program_id(0) == 0)
    def _():
        qi = lax.broadcasted_iota(jnp.int32, (slots, slots), 0)
        ki = lax.broadcasted_iota(jnp.int32, (slots, slots), 1)
        allowed = (segc_ref[...] == segr_ref[...]) & (ki <= qi)
        allowed = allowed & ((qi - ki < WINDOW) | (posr_ref[...] < SINK))
        bias_ref[...] = jnp.where(allowed, 0.0, -jnp.inf).astype(jnp.float32)

    cosine = cos_ref[...]
    sine = sin_ref[...]
    src = lax.broadcasted_iota(jnp.int32, (LANES, LANES), 0)
    dst = lax.broadcasted_iota(jnp.int32, (LANES, LANES), 1)
    first = dst % HEAD_SIZE < HEAD_SIZE // 2
    turn = jnp.where(
        first & (src == dst + HEAD_SIZE // 2), -1.0, jnp.where(~first & (src == dst - HEAD_SIZE // 2), 1.0, 0.0)
    ).astype(jnp.bfloat16)

    def rotate(x):
        turned = jnp.dot(x, turn, preferred_element_type=jnp.float32)
        return (x.astype(jnp.float32) * cosine + turned * sine).astype(jnp.bfloat16)

    q_rot = rotate(q_ref[...]) * jnp.bfloat16(1.0 / math.sqrt(HEAD_SIZE))
    k_rot = rotate(k_ref[...])
    v = v_ref[...]
    lane = lax.broadcasted_iota(jnp.int32, (1, LANES), 1)
    low = lane < HEAD_SIZE
    zero = jnp.zeros((), jnp.bfloat16)
    q_low = jnp.where(low, q_rot, zero)
    q_high = jnp.where(low, zero, q_rot)
    for i in range(slots // block):
        keys = block * (i + 1)
        k_part = k_rot[:keys]
        v_part = v[:keys]
        bias = bias_ref[i * block:(i + 1) * block, :keys]
        parts = []
        for qh in (q_low, q_high):
            scores = lax.dot_general(
                qh[i * block:(i + 1) * block], k_part, (((1,), (1,)), ((), ())),
                preferred_element_type=jnp.float32,
            )
            scores = scores + bias
            largest = jnp.max(scores, axis=-1, keepdims=True)
            raised = jnp.exp(scores - largest)
            total = jnp.sum(raised, axis=-1, keepdims=True)
            weights = (raised * (1.0 / total)).astype(jnp.bfloat16)
            parts.append(jnp.dot(weights, v_part, preferred_element_type=jnp.float32))
        context = jnp.where(low, parts[0], parts[1]).astype(jnp.bfloat16)
        ctx_ref[pl.program_id(0), i * block:(i + 1) * block, :] = context

    @pl.when(pl.program_id(0) == pl.num_programs(0) - 1)
    def _():
        heads = jnp.concatenate([ctx_ref[t] for t in range(ctx_ref.shape[0])], axis=1)
        mixed = h_ref[...].astype(jnp.float32) + jnp.dot(
            heads, w_ref[...], preferred_element_type=jnp.float32
        )
        out_ref[...] = mixed.astype(out_ref.dtype)


def attend(queries, projected_keys, projected_values, segment, out_weight, hidden_in):
    slot_capacity = queries.shape[0]
    slots = jnp.arange(slot_capacity, dtype=jnp.int32)
    begins = jnp.concatenate([jnp.ones((1,), dtype=jnp.bool_), segment[1:] != segment[:-1]])
    starts = lax.cummax(jnp.where(begins, slots, 0), axis=0)
    token_position = slots - starts
    cosine, sine = rotation_tables(token_position)
    def doubled(x):
        x = x.reshape(slot_capacity, KEY_VALUE_HEADS, 1, HEAD_SIZE)
        x = jnp.broadcast_to(x, (slot_capacity, KEY_VALUE_HEADS, 2, HEAD_SIZE))
        return x.reshape(slot_capacity, KEY_VALUE_HEADS * 2 * HEAD_SIZE)
    keys2 = doubled(projected_keys)
    values2 = doubled(projected_values)
    tiles = QUERY_HEADS * HEAD_SIZE // LANES
    per_kv = tiles // KEY_VALUE_HEADS
    full = lambda t: (0, 0)
    width = out_weight.shape[1]
    return pl.pallas_call(
        attention_kernel,
        grid=(tiles,),
        in_specs=[
            pl.BlockSpec((slot_capacity, LANES), lambda t: (0, t)),
            pl.BlockSpec((slot_capacity, LANES), lambda t: (0, t // per_kv)),
            pl.BlockSpec((slot_capacity, LANES), lambda t: (0, t // per_kv)),
            pl.BlockSpec((slot_capacity, LANES), full),
            pl.BlockSpec((slot_capacity, LANES), full),
            pl.BlockSpec((slot_capacity, 1), full),
            pl.BlockSpec((1, slot_capacity), full),
            pl.BlockSpec((1, slot_capacity), full),
            pl.BlockSpec((width, width), full),
            pl.BlockSpec((slot_capacity, width), full),
        ],
        out_specs=pl.BlockSpec((slot_capacity, width), full),
        out_shape=jax.ShapeDtypeStruct((slot_capacity, width), jnp.bfloat16),
        scratch_shapes=[
            pltpu.VMEM((slot_capacity, slot_capacity), jnp.float32),
            pltpu.VMEM((tiles, slot_capacity, LANES), jnp.bfloat16),
        ],
        compiler_params=pltpu.CompilerParams(dimension_semantics=("arbitrary",)),
    )(
        queries, keys2, values2, cosine, sine,
        segment.reshape(slot_capacity, 1), segment.reshape(1, slot_capacity),
        token_position.reshape(1, slot_capacity), out_weight, hidden_in,
    )


def normalize(rows, norm_gain):
    numbers = rows.astype(jnp.float32)
    factor = lax.rsqrt(jnp.mean(numbers * numbers, axis=-1, keepdims=True) + norm_eps)
    return (numbers * factor * norm_gain[None, :]).astype(jnp.bfloat16)


def project(attended_context, hidden_in, out_weight):
    return (
        hidden_in.astype(jnp.float32)
        + jnp.dot(attended_context, out_weight, preferred_element_type=jnp.float32)
    ).astype(jnp.bfloat16)


def ffn_kernel(*refs):
    *x_refs, g_ref, u_ref, d_ref, o_ref = refs
    x = jnp.concatenate([r[...] for r in x_refs], axis=0) if len(x_refs) > 1 else x_refs[0][...]
    gate = jnp.dot(x, g_ref[...], preferred_element_type=jnp.float32)
    upward = jnp.dot(x, u_ref[...], preferred_element_type=jnp.float32)
    hidden = (gate / (1.0 + jnp.exp(-gate)) * upward).astype(jnp.bfloat16)
    o_ref[...] = jnp.dot(hidden, d_ref[...], preferred_element_type=jnp.float32).astype(o_ref.dtype)


def ffn_rows(blocks, gate_weight, up_weight, down_weight):
    width = blocks[0].shape[1]
    count = sum(b.shape[0] for b in blocks)
    units = gate_weight.shape[1]
    flops = 6 * count * width * units
    moved = 2 * (3 * width * units + 2 * count * width)
    return pl.pallas_call(
        ffn_kernel,
        grid=(1,),
        in_specs=[pl.BlockSpec(b.shape, lambda j: (0, 0)) for b in blocks] + [
            pl.BlockSpec((width, units), lambda j: (0, 0)),
            pl.BlockSpec((width, units), lambda j: (0, 0)),
            pl.BlockSpec((units, width), lambda j: (0, 0)),
        ],
        out_specs=pl.BlockSpec((count, width), lambda j: (0, 0)),
        out_shape=jax.ShapeDtypeStruct((count, width), jnp.bfloat16),
        compiler_params=pltpu.CompilerParams(dimension_semantics=("arbitrary",)),
        cost_estimate=pl.CostEstimate(flops=flops, transcendentals=count * units, bytes_accessed=moved),
    )(*blocks, gate_weight, up_weight, down_weight)


def feed_forward(normed, gate_weight, up_weight, down_weight):
    groups = lax.axis_size("grp")
    rows = normed.shape[0]
    arrived = [
        lax.ppermute(normed, "grp", [(j, (j + k) % groups) for j in range(groups)])
        for k in range(1, groups)
    ]
    own = ffn_rows([normed], gate_weight, up_weight, down_weight)
    own, *arrived = lax.optimization_barrier((own, *arrived))
    others = ffn_rows(arrived, gate_weight, up_weight, down_weight)
    total = own.astype(jnp.float32)
    for k in range(1, groups):
        part = others[(k - 1) * rows:k * rows]
        part = lax.ppermute(part, "grp", [(j, (j - k) % groups) for j in range(groups)])
        total = total + part.astype(jnp.float32)
    return total


def take_rows(table, index, valid):
    columns = jnp.arange(table.shape[0], dtype=jnp.int32)
    chosen = (index[:, None] == columns[None, :]) & valid[:, None]
    return jnp.dot(
        chosen.astype(table.dtype), table, preferred_element_type=jnp.float32
    ).astype(table.dtype)


def on_device(
    hidden_in,
    queries,
    projected_keys,
    projected_values,
    segment,
    live_rows,
    out_weight,
    norm_gain,
    gate_weight,
    up_weight,
    down_weight,
):
    slot_capacity = hidden_in.shape[0]
    rows = attend(
        queries, projected_keys, projected_values, segment.reshape(slot_capacity), out_weight, hidden_in
    )
    slots = jnp.arange(slot_capacity, dtype=jnp.int32)
    own_count = live_rows.reshape(())
    request_owners = lax.axis_size("req")
    own_index = lax.axis_index("req")
    block_rows = slot_capacity // request_owners
    counts = lax.all_to_all(
        jnp.broadcast_to(live_rows.reshape(1, 1), (request_owners, LANES)), "req", 0, 0, tiled=True
    )[:, 0]
    ends = jnp.cumsum(counts)
    firsts = ends - counts
    owner_ids = jnp.arange(request_owners, dtype=jnp.int32)
    own_first = jnp.sum(jnp.where(owner_ids == own_index, firsts, 0))
    own_shift = own_first % request_owners
    stream = jnp.arange(BAL, dtype=jnp.int32) * request_owners + own_index
    source = jnp.sum((ends[None, :] <= stream[:, None]).astype(jnp.int32), axis=1)
    source_first = jnp.sum(
        jnp.where(source[:, None] == owner_ids[None, :], firsts[None, :], 0), axis=1
    )
    pick = source * block_rows + (stream - source_first) // request_owners
    dest = jnp.arange(request_owners, dtype=jnp.int32)[:, None]
    blocks = jnp.arange(block_rows, dtype=jnp.int32)[None, :]
    send_row = blocks * request_owners + (dest - own_shift) % request_owners
    send_row = send_row.reshape(slot_capacity)
    outbound = take_rows(rows, send_row, send_row < own_count)
    arrived = lax.all_to_all(
        outbound.reshape(request_owners, block_rows, -1), "req", 0, 0, tiled=True
    )
    mixed = take_rows(arrived.reshape(slot_capacity, -1), pick, pick >= 0)
    normed = normalize(mixed, norm_gain)
    result = (
        mixed.astype(jnp.float32) + feed_forward(normed, gate_weight, up_weight, down_weight)
    ).astype(jnp.bfloat16)
    lanes = (own_index - firsts) % request_owners
    source_row = jnp.arange(block_rows, dtype=jnp.int32)[:, None] * request_owners + lanes[None, :]
    valid = source_row < counts[None, :]
    target = jnp.where(valid, (firsts[None, :] + source_row) // request_owners, 0)
    outgoing = take_rows(result, target.T.reshape(slot_capacity), valid.T.reshape(slot_capacity))
    returned = lax.all_to_all(
        outgoing.reshape(request_owners, block_rows, -1), "req", 0, 0, tiled=True
    ).reshape(slot_capacity, -1)
    back_row = ((slots % request_owners + own_shift) % request_owners) * block_rows + slots // request_owners
    return take_rows(returned, back_row, back_row >= 0)


def solution(mesh):
    placed = (
        P(("req", "grp"), None),
        P(("req", "grp"), None),
        P(("req", "grp"), None),
        P(("req", "grp"), None),
        P("req", "grp", None),
        P("req", "grp"),
        P(),
        P(),
        P(None, "grp"),
        P(None, "grp"),
        P("grp", None),
    )
    return jax.shard_map(
        on_device, mesh=mesh, in_specs=placed, out_specs=P(("req", "grp"), None), check_vma=False
    )
```

```python
import math

import jax
import jax.numpy as jnp
from jax import lax
from jax.experimental import pallas as pl
from jax.experimental.pallas import tpu as pltpu
from jax.sharding import PartitionSpec as P

QUERY_HEADS = 20
KEY_VALUE_HEADS = 5
HEAD_SIZE = 64
WINDOW = 128
SINK = 4
BAL = 128


rope_base = 10000.0
norm_eps = 1e-05
LANES = 128


def rotation_tables(token_position):
    half = HEAD_SIZE // 2
    inverse = rope_base ** (-(2.0 * jnp.arange(half, dtype=jnp.float32)) / HEAD_SIZE)
    angle = token_position.astype(jnp.float32)[:, None] * inverse[None, :]
    reps = LANES // half
    return jnp.tile(jnp.cos(angle), (1, reps)), jnp.tile(jnp.sin(angle), (1, reps))


def half_turn_matrix():
    lane = jnp.arange(LANES, dtype=jnp.int32)
    local = lane % HEAD_SIZE
    half = HEAD_SIZE // 2
    src = jnp.where(local < half, lane + half, lane - half)
    sign = jnp.where(local < half, -1.0, 1.0)
    turn = jnp.where(lane[:, None] == src[None, :], sign[None, :], 0.0)
    return turn.astype(jnp.bfloat16)


def attention_kernel(q_ref, k_ref, v_ref, cos_ref, sin_ref, segc_ref, segr_ref, posr_ref, w_ref, h_ref, out_ref, bias_ref, ctx_ref):
    slots = q_ref.shape[0]
    block = LANES

    @pl.when(pl.program_id(0) == 0)
    def _():
        qi = lax.broadcasted_iota(jnp.int32, (slots, slots), 0)
        ki = lax.broadcasted_iota(jnp.int32, (slots, slots), 1)
        allowed = (segc_ref[...] == segr_ref[...]) & (ki <= qi)
        allowed = allowed & ((qi - ki < WINDOW) | (posr_ref[...] < SINK))
        bias_ref[...] = jnp.where(allowed, 0.0, -jnp.inf).astype(jnp.float32)

    cosine = cos_ref[...]
    sine = sin_ref[...]
    src = lax.broadcasted_iota(jnp.int32, (LANES, LANES), 0)
    dst = lax.broadcasted_iota(jnp.int32, (LANES, LANES), 1)
    first = dst % HEAD_SIZE < HEAD_SIZE // 2
    turn = jnp.where(
        first & (src == dst + HEAD_SIZE // 2), -1.0, jnp.where(~first & (src == dst - HEAD_SIZE // 2), 1.0, 0.0)
    ).astype(jnp.bfloat16)

    def rotate(x):
        turned = jnp.dot(x, turn, preferred_element_type=jnp.float32)
        return (x.astype(jnp.float32) * cosine + turned * sine).astype(jnp.bfloat16)

    q_rot = rotate(q_ref[...]) * jnp.bfloat16(1.0 / math.sqrt(HEAD_SIZE))
    k_rot = rotate(k_ref[...])
    v = v_ref[...]
    lane = lax.broadcasted_iota(jnp.int32, (1, LANES), 1)
    low = lane < HEAD_SIZE
    zero = jnp.zeros((), jnp.bfloat16)
    q_low = jnp.where(low, q_rot, zero)
    q_high = jnp.where(low, zero, q_rot)
    for i in range(slots // block):
        keys = block * (i + 1)
        k_part = k_rot[:keys]
        v_part = v[:keys]
        bias = bias_ref[i * block:(i + 1) * block, :keys]
        parts = []
        for qh in (q_low, q_high):
            scores = lax.dot_general(
                qh[i * block:(i + 1) * block], k_part, (((1,), (1,)), ((), ())),
                preferred_element_type=jnp.float32,
            )
            scores = scores + bias
            largest = jnp.max(scores, axis=-1, keepdims=True)
            raised = jnp.exp(scores - largest)
            total = jnp.sum(raised, axis=-1, keepdims=True)
            weights = (raised * (1.0 / total)).astype(jnp.bfloat16)
            parts.append(jnp.dot(weights, v_part, preferred_element_type=jnp.float32))
        context = jnp.where(low, parts[0], parts[1]).astype(jnp.bfloat16)
        ctx_ref[pl.program_id(0), i * block:(i + 1) * block, :] = context

    @pl.when(pl.program_id(0) == pl.num_programs(0) - 1)
    def _():
        heads = jnp.concatenate([ctx_ref[t] for t in range(ctx_ref.shape[0])], axis=1)
        mixed = h_ref[...].astype(jnp.float32) + jnp.dot(
            heads, w_ref[...], preferred_element_type=jnp.float32
        )
        out_ref[...] = mixed.astype(out_ref.dtype)


def attend(queries, projected_keys, projected_values, segment, out_weight, hidden_in):
    slot_capacity = queries.shape[0]
    slots = jnp.arange(slot_capacity, dtype=jnp.int32)
    begins = jnp.concatenate([jnp.ones((1,), dtype=jnp.bool_), segment[1:] != segment[:-1]])
    starts = lax.cummax(jnp.where(begins, slots, 0), axis=0)
    token_position = slots - starts
    cosine, sine = rotation_tables(token_position)
    def doubled(x):
        x = x.reshape(slot_capacity, KEY_VALUE_HEADS, 1, HEAD_SIZE)
        x = jnp.broadcast_to(x, (slot_capacity, KEY_VALUE_HEADS, 2, HEAD_SIZE))
        return x.reshape(slot_capacity, KEY_VALUE_HEADS * 2 * HEAD_SIZE)
    keys2 = doubled(projected_keys)
    values2 = doubled(projected_values)
    tiles = QUERY_HEADS * HEAD_SIZE // LANES
    per_kv = tiles // KEY_VALUE_HEADS
    full = lambda t: (0, 0)
    width = out_weight.shape[1]
    return pl.pallas_call(
        attention_kernel,
        grid=(tiles,),
        in_specs=[
            pl.BlockSpec((slot_capacity, LANES), lambda t: (0, t)),
            pl.BlockSpec((slot_capacity, LANES), lambda t: (0, t // per_kv)),
            pl.BlockSpec((slot_capacity, LANES), lambda t: (0, t // per_kv)),
            pl.BlockSpec((slot_capacity, LANES), full),
            pl.BlockSpec((slot_capacity, LANES), full),
            pl.BlockSpec((slot_capacity, 1), full),
            pl.BlockSpec((1, slot_capacity), full),
            pl.BlockSpec((1, slot_capacity), full),
            pl.BlockSpec((width, width), full),
            pl.BlockSpec((slot_capacity, width), full),
        ],
        out_specs=pl.BlockSpec((slot_capacity, width), full),
        out_shape=jax.ShapeDtypeStruct((slot_capacity, width), jnp.bfloat16),
        scratch_shapes=[
            pltpu.VMEM((slot_capacity, slot_capacity), jnp.float32),
            pltpu.VMEM((tiles, slot_capacity, LANES), jnp.bfloat16),
        ],
        compiler_params=pltpu.CompilerParams(dimension_semantics=("arbitrary",)),
    )(
        queries, keys2, values2, cosine, sine,
        segment.reshape(slot_capacity, 1), segment.reshape(1, slot_capacity),
        token_position.reshape(1, slot_capacity), out_weight, hidden_in,
    )


def normalize(rows, norm_gain):
    numbers = rows.astype(jnp.float32)
    factor = lax.rsqrt(jnp.mean(numbers * numbers, axis=-1, keepdims=True) + norm_eps)
    return (numbers * factor * norm_gain[None, :]).astype(jnp.bfloat16)


def project(attended_context, hidden_in, out_weight):
    return (
        hidden_in.astype(jnp.float32)
        + jnp.dot(attended_context, out_weight, preferred_element_type=jnp.float32)
    ).astype(jnp.bfloat16)


def ffn_kernel(*refs):
    *x_refs, g_ref, u_ref, d_ref, o_ref = refs
    x = jnp.concatenate([r[...] for r in x_refs], axis=0) if len(x_refs) > 1 else x_refs[0][...]
    gate = jnp.dot(x, g_ref[...], preferred_element_type=jnp.float32)
    upward = jnp.dot(x, u_ref[...], preferred_element_type=jnp.float32)
    hidden = (gate / (1.0 + jnp.exp(-gate)) * upward).astype(jnp.bfloat16)
    o_ref[...] = jnp.dot(hidden, d_ref[...], preferred_element_type=jnp.float32).astype(o_ref.dtype)


def ffn_rows(blocks, gate_weight, up_weight, down_weight):
    width = blocks[0].shape[1]
    count = sum(b.shape[0] for b in blocks)
    units = gate_weight.shape[1]
    flops = 6 * count * width * units
    moved = 2 * (3 * width * units + 2 * count * width)
    return pl.pallas_call(
        ffn_kernel,
        grid=(1,),
        in_specs=[pl.BlockSpec(b.shape, lambda j: (0, 0)) for b in blocks] + [
            pl.BlockSpec((width, units), lambda j: (0, 0)),
            pl.BlockSpec((width, units), lambda j: (0, 0)),
            pl.BlockSpec((units, width), lambda j: (0, 0)),
        ],
        out_specs=pl.BlockSpec((count, width), lambda j: (0, 0)),
        out_shape=jax.ShapeDtypeStruct((count, width), jnp.bfloat16),
        compiler_params=pltpu.CompilerParams(dimension_semantics=("arbitrary",)),
        cost_estimate=pl.CostEstimate(flops=flops, transcendentals=count * units, bytes_accessed=moved),
    )(*blocks, gate_weight, up_weight, down_weight)


def feed_forward(normed, gate_weight, up_weight, down_weight):
    groups = lax.axis_size("grp")
    rows = normed.shape[0]
    arrived = [
        lax.ppermute(normed, "grp", [(j, (j + k) % groups) for j in range(groups)])
        for k in range(1, groups)
    ]
    own = ffn_rows([normed], gate_weight, up_weight, down_weight)
    own, *arrived = lax.optimization_barrier((own, *arrived))
    others = ffn_rows(arrived, gate_weight, up_weight, down_weight)
    total = own.astype(jnp.float32)
    for k in range(1, groups):
        part = others[(k - 1) * rows:k * rows]
        part = lax.ppermute(part, "grp", [(j, (j - k) % groups) for j in range(groups)])
        total = total + part.astype(jnp.float32)
    return total


def take_rows(table, index, valid):
    columns = jnp.arange(table.shape[0], dtype=jnp.int32)
    chosen = (index[:, None] == columns[None, :]) & valid[:, None]
    return jnp.dot(
        chosen.astype(table.dtype), table, preferred_element_type=jnp.float32
    ).astype(table.dtype)


def on_device(
    hidden_in,
    queries,
    projected_keys,
    projected_values,
    segment,
    live_rows,
    out_weight,
    norm_gain,
    gate_weight,
    up_weight,
    down_weight,
):
    slot_capacity = hidden_in.shape[0]
    rows = attend(
        queries, projected_keys, projected_values, segment.reshape(slot_capacity), out_weight, hidden_in
    )
    slots = jnp.arange(slot_capacity, dtype=jnp.int32)
    own_count = live_rows.reshape(())
    request_owners = lax.axis_size("req")
    own_index = lax.axis_index("req")
    block_rows = slot_capacity // request_owners
    counts = lax.all_to_all(
        jnp.broadcast_to(live_rows.reshape(1, 1), (request_owners, 8)), "req", 0, 0, tiled=True
    )[:, 0]
    ends = jnp.cumsum(counts)
    firsts = ends - counts
    owner_ids = jnp.arange(request_owners, dtype=jnp.int32)
    own_first = jnp.sum(jnp.where(owner_ids == own_index, firsts, 0))
    own_shift = own_first % request_owners
    stream = jnp.arange(BAL, dtype=jnp.int32) * request_owners + own_index
    source = jnp.sum((ends[None, :] <= stream[:, None]).astype(jnp.int32), axis=1)
    source_first = jnp.sum(
        jnp.where(source[:, None] == owner_ids[None, :], firsts[None, :], 0), axis=1
    )
    pick = source * block_rows + (stream - source_first) // request_owners
    dest = jnp.arange(request_owners, dtype=jnp.int32)[:, None]
    blocks = jnp.arange(block_rows, dtype=jnp.int32)[None, :]
    send_row = blocks * request_owners + (dest - own_shift) % request_owners
    send_row = send_row.reshape(slot_capacity)
    outbound = take_rows(rows, send_row, send_row < own_count)
    arrived = lax.all_to_all(
        outbound.reshape(request_owners, block_rows, -1), "req", 0, 0, tiled=True
    )
    mixed = take_rows(arrived.reshape(slot_capacity, -1), pick, pick >= 0)
    normed = normalize(mixed, norm_gain)
    result = (
        mixed.astype(jnp.float32) + feed_forward(normed, gate_weight, up_weight, down_weight)
    ).astype(jnp.bfloat16)
    lanes = (own_index - firsts) % request_owners
    source_row = jnp.arange(block_rows, dtype=jnp.int32)[:, None] * request_owners + lanes[None, :]
    valid = source_row < counts[None, :]
    target = jnp.where(valid, (firsts[None, :] + source_row) // request_owners, 0)
    outgoing = take_rows(result, target.T.reshape(slot_capacity), valid.T.reshape(slot_capacity))
    returned = lax.all_to_all(
        outgoing.reshape(request_owners, block_rows, -1), "req", 0, 0, tiled=True
    ).reshape(slot_capacity, -1)
    back_row = ((slots % request_owners + own_shift) % request_owners) * block_rows + slots // request_owners
    return take_rows(returned, back_row, back_row >= 0)


def solution(mesh):
    placed = (
        P(("req", "grp"), None),
        P(("req", "grp"), None),
        P(("req", "grp"), None),
        P(("req", "grp"), None),
        P("req", "grp", None),
        P("req", "grp"),
        P(),
        P(),
        P(None, "grp"),
        P(None, "grp"),
        P("grp", None),
    )
    return jax.shard_map(
        on_device, mesh=mesh, in_specs=placed, out_specs=P(("req", "grp"), None), check_vma=False
    )
```
